32 devices in a mesh: space: 16 (over z, y, x), tm: 2 (over core).
Axes of the slice: x: 2, y: 2, z: 4, core: 2. Of those that a mesh axis runs over, the one named last changes fastest.
Arguments:
- initial: float32 [32, 256, 128], P('space'), may hold values from -6 to 6
- guesses: float32 [2, 32, 256, 128], P('tm', 'space'), may hold values from -6 to 6
- diffusivity: float32 [32, 256, 128], P('space'), may hold values from 0.4 to 1.2
- reaction: float32 [32, 256, 128], P('space'), may hold values from 0.1 to 1
Outputs:
- corrected: float32 [2, 32, 256, 128], P('tm', 'space')
- residual: float32 [2, 32, 256, 128], P('tm', 'space')
The draws below stay inside these ranges and needn't reach their ends.
All inputs are finite; a program needn't handle non-finite values.
Results may differ from the reference program's by a relative error of at most 0.0001.
Values sent between devices are 32-bit elements; how exact they have to be, the bound alone decides.
No kernel may reach another device: no remote copies, remote signals or barrier semaphores. Data moves between devices by JAX's collectives and lax.ppermute only.
A program may use at most 64 MiB of HBM per device.

```python
import math
import jax
import jax.numpy as jnp
from jax import lax

NY = 256
NZ = 128
STEPS = 4
NX = 32
INTERVALS = 2


def steps_of(key, extent, cuts, low, largest):
    def one(position, parts):
        steps = jax.random.uniform(jax.random.fold_in(jax.random.fold_in(key, 6), position), (parts,), jnp.float32, low / len(cuts), largest / len(cuts))
        return jnp.repeat(jnp.exp(steps), extent[position] // parts).reshape((-1,) + (1,) * (len(extent) - position - 1))

    level = one(*cuts[0])
    for cut in cuts[1:]:
        level = level * one(*cut)
    return level


def gaussian(key, shape, scale, limit, pieces=(), held_as=jnp.bfloat16):
    entries = scale * jax.random.normal(key, shape, jnp.float32)
    if pieces:
        entries = entries * steps_of(key, shape, pieces, -0.22, 0.18)
    return jnp.clip(entries, -limit, limit).astype(held_as)


def setup_inputs(seed: int = 0) -> dict:
    key_list = jax.random.split(jax.random.key(seed), 5)
    initial = gaussian(key_list[0], (NX, NY, NZ), 1.0, 6.0, ((0, 16),), jnp.float32)
    guesses = gaussian(key_list[1], (INTERVALS, NX, NY, NZ), 1.0, 6.0, ((0, 2), (1, 16)), jnp.float32)
    diffusivity = jnp.clip(jnp.exp(math.log(1.2) - 1.0986123 * jax.random.uniform(key_list[2], (NX, NY, NZ), jnp.float32) ** steps_of(key_list[2], (NX, NY, NZ), ((0, 16),), -0.2, 0.2)), 0.4, 1.2)
    reaction = jnp.clip(jnp.exp(math.log(1.0) - 2.3025851 * jax.random.uniform(key_list[3], (NX, NY, NZ), jnp.float32) ** steps_of(key_list[3], (NX, NY, NZ), ((0, 16),), -0.2, 0.2)), 0.1, 1.0)
    return {"initial": initial, "guesses": guesses, "diffusivity": diffusivity, "reaction": reaction}


def advance(field, conduct, absorb, diffuse_scale, react_scale):
    center = field[1:-1]
    middle = conduct[1:-1]
    padded = jnp.pad(center, ((0, 0), (1, 1), (1, 1)))
    conduct_pad = jnp.pad(middle, ((0, 0), (1, 1), (1, 1)))
    inflow = 0.5 * (conduct[2:] + middle) * (field[2:] - center)
    inflow = inflow + 0.5 * (conduct[:-2] + middle) * (field[:-2] - center)
    inflow = inflow + 0.5 * (conduct_pad[:, 2:, 1:-1] + middle) * (padded[:, 2:, 1:-1] - center)
    inflow = inflow + 0.5 * (conduct_pad[:, :-2, 1:-1] + middle) * (padded[:, :-2, 1:-1] - center)
    inflow = inflow + 0.5 * (conduct_pad[:, 1:-1, 2:] + middle) * (padded[:, 1:-1, 2:] - center)
    inflow = inflow + 0.5 * (conduct_pad[:, 1:-1, :-2] + middle) * (padded[:, 1:-1, :-2] - center)
    return center + diffuse_scale * inflow - react_scale * absorb[1:-1] * center


def plane_pad(field):
    return jnp.pad(field, ((1, 1), (0, 0), (0, 0)))


def propagate(start, conduct, absorb, diffuse_scale, react_scale, count):
    conduct_pad = plane_pad(conduct)
    absorb_pad = plane_pad(absorb)
    field = start
    for number in range(count):
        field = advance(plane_pad(field), conduct_pad, absorb_pad, diffuse_scale, react_scale)
    return field


def restrict(field):
    first, second, third = field.shape
    blocks = field.reshape(first // 2, 2, second // 2, 2, third // 2, 2)
    return jnp.mean(blocks, axis=(1, 3, 5))


def prolong(field):
    first, second, third = field.shape
    spread = jnp.broadcast_to(field[:, None, :, None, :, None], (first, 2, second, 2, third, 2))
    return spread.reshape(first * 2, second * 2, third * 2)


def reference(initial, guesses, diffusivity, reaction):
    def fine_prop(start):
        return propagate(start, diffusivity, reaction, 0.1, 0.1, STEPS)

    advanced = lax.map(fine_prop, guesses)
    relaxed = jnp.concatenate([initial[None], advanced[:-1]], axis=0)
    residual = lax.map(fine_prop, relaxed) - advanced
    coarse_cond = restrict(diffusivity)
    coarse_rate = restrict(reaction)

    def chain(carry, term):
        carry = propagate(carry, coarse_cond, coarse_rate, 0.1, 0.4, STEPS // 4) + restrict(term)
        return carry, carry

    zero_error = jnp.zeros(coarse_cond.shape, jnp.float32)
    final_error, errors = lax.scan(chain, zero_error, residual)
    corrected = advanced + lax.map(prolong, errors)
    return corrected, residual
```

```python
import jax
import jax.numpy as jnp
import numpy as np
from jax import lax
from jax.sharding import PartitionSpec as P

STEPS = 4
COARSE_STEPS = STEPS // 4


def advance(field, conduct, absorb, diffuse_scale, react_scale):
    center = field[1:-1]
    middle = conduct[1:-1]
    padded = jnp.pad(center, ((0, 0), (1, 1), (1, 1)))
    conduct_pad = jnp.pad(middle, ((0, 0), (1, 1), (1, 1)))
    inflow = 0.5 * (conduct[2:] + middle) * (field[2:] - center)
    inflow = inflow + 0.5 * (conduct[:-2] + middle) * (field[:-2] - center)
    inflow = inflow + 0.5 * (conduct_pad[:, 2:, 1:-1] + middle) * (padded[:, 2:, 1:-1] - center)
    inflow = inflow + 0.5 * (conduct_pad[:, :-2, 1:-1] + middle) * (padded[:, :-2, 1:-1] - center)
    inflow = inflow + 0.5 * (conduct_pad[:, 1:-1, 2:] + middle) * (padded[:, 1:-1, 2:] - center)
    inflow = inflow + 0.5 * (conduct_pad[:, 1:-1, :-2] + middle) * (padded[:, 1:-1, :-2] - center)
    return center + diffuse_scale * inflow - react_scale * absorb[1:-1] * center


def pair_matrix(fine):
    rows = np.arange(fine)[:, None] // 2 == np.arange(fine // 2)[None, :]
    return jnp.asarray(rows.astype(np.float32))


def restrict(field):
    first, second, third = field.shape
    planes = field.reshape(first // 2, 2, second, third).sum(axis=1)
    rows = pair_matrix(second)
    cols = pair_matrix(third)
    out = jnp.einsum("Yy,mYZ,Zz->myz", rows, planes, cols, precision=lax.Precision.HIGHEST)
    return out * 0.125


def prolong(field):
    first, second, third = field.shape
    rows = pair_matrix(second * 2)
    cols = pair_matrix(third * 2)
    out = jnp.einsum("Yy,myz,Zz->mYZ", rows, field, cols, precision=lax.Precision.HIGHEST)
    return jnp.repeat(out, 2, axis=0)


def gather_planes(block, axis_names, pairs_of, distances):
    pieces = {}
    for d in distances:
        if d == 0 and pairs_of(0) is None:
            pieces[d] = block
            continue
        pieces[d] = lax.ppermute(block, axis_names, pairs_of(d))
    return pieces


def shards(initial, guesses, diffusivity, reaction):
    space = lax.axis_size("space")
    times = lax.axis_size("tm")
    me_s = lax.axis_index("space")
    me_t = lax.axis_index("tm")
    n = initial.shape[0]
    halo = STEPS
    reach = -(-halo // n)

    def space_pairs(d):
        return [(s + d, s) for s in range(space) if 0 <= s + d < space]

    def joint(s, t):
        return s * times + t

    def prev_pairs(d):
        return [
            (joint(s + d, (t - 1) % times), joint(s, t))
            for s in range(space)
            for t in range(times)
            if 0 <= s + d < space
        ]

    start = guesses[0]
    local = jnp.stack([diffusivity, reaction, start])
    distances = [d for d in range(-reach, reach + 1)]
    got = gather_planes(local, "space", lambda d: None if d == 0 else space_pairs(d), distances)
    wide = jnp.concatenate([got[d] for d in distances], axis=1)
    lo = reach * n - halo
    hi = reach * n + n + halo
    wide = wide[:, lo:hi]
    conduct, absorb, field0 = wide[0], wide[1], wide[2]
    plane_ids = me_s * n - halo + jnp.arange(n + 2 * halo)
    inside = ((plane_ids >= 0) & (plane_ids < space * n)).astype(jnp.float32)[:, None, None]

    def fine_prop(field):
        for number in range(STEPS):
            cut = number
            k = conduct[cut : conduct.shape[0] - cut]
            c = absorb[cut : absorb.shape[0] - cut]
            field = advance(field, k, c, 0.1, 0.1)
            if number < STEPS - 1:
                m = inside[cut + 1 : inside.shape[0] - cut - 1]
                field = jnp.where(m > 0, field, 0.0)
        return field

    advanced = fine_prop(field0)
    payload = jnp.where(me_t == times - 1, initial, advanced)
    got2 = gather_planes(payload, ("space", "tm"), prev_pairs, distances)
    relaxed = jnp.concatenate([got2[d] for d in distances], axis=0)[lo:hi]
    residual = fine_prop(relaxed) - advanced

    cn = n // 2
    creach = -(-1 // cn)
    cdist = [d for d in range(-creach, creach + 1)]
    coarse_k = restrict(conduct[halo - 2 * creach * cn : halo + n + 2 * creach * cn])
    coarse_c = restrict(absorb[halo - 2 * creach * cn : halo + n + 2 * creach * cn])
    ck = coarse_k[creach * cn - 1 : creach * cn + cn + 1]
    cc = coarse_c[creach * cn - 1 : creach * cn + cn + 1]
    source = restrict(residual)

    def chain_pairs(d):
        return [
            (joint(s + d, t - 1), joint(s, t))
            for s in range(space)
            for t in range(1, times)
            if 0 <= s + d < space
        ]

    partial_error = source
    for turn in range(times - 1):
        got3 = gather_planes(partial_error, ("space", "tm"), chain_pairs, cdist)
        behind = jnp.concatenate([got3[d] for d in cdist], axis=0)
        behind = behind[creach * cn - 1 : creach * cn + cn + 1]
        for number in range(COARSE_STEPS):
            behind = advance(behind, ck, cc, 0.1, 0.4)
        partial_error = source + behind
    corrected = advanced + prolong(partial_error)
    return (corrected[None], residual[None])


def solution(mesh):
    in_specs = (
        P("space", None, None),
        P("tm", "space", None, None),
        P("space", None, None),
        P("space", None, None),
    )
    out_specs = (P("tm", "space", None, None), P("tm", "space", None, None))
    return jax.shard_map(shards, mesh=mesh, in_specs=in_specs, out_specs=out_specs, check_vma=False)
```

```python
import jax
import jax.numpy as jnp
import numpy as np
from jax import lax
from jax.sharding import PartitionSpec as P

STEPS = 4
COARSE_STEPS = STEPS // 4


def advance(field, conduct, absorb, diffuse_scale, react_scale):
    center = field[1:-1]
    middle = conduct[1:-1]
    padded = jnp.pad(center, ((0, 0), (1, 1), (1, 1)))
    conduct_pad = jnp.pad(middle, ((0, 0), (1, 1), (1, 1)))
    inflow = 0.5 * (conduct[2:] + middle) * (field[2:] - center)
    inflow = inflow + 0.5 * (conduct[:-2] + middle) * (field[:-2] - center)
    inflow = inflow + 0.5 * (conduct_pad[:, 2:, 1:-1] + middle) * (padded[:, 2:, 1:-1] - center)
    inflow = inflow + 0.5 * (conduct_pad[:, :-2, 1:-1] + middle) * (padded[:, :-2, 1:-1] - center)
    inflow = inflow + 0.5 * (conduct_pad[:, 1:-1, 2:] + middle) * (padded[:, 1:-1, 2:] - center)
    inflow = inflow + 0.5 * (conduct_pad[:, 1:-1, :-2] + middle) * (padded[:, 1:-1, :-2] - center)
    return center + diffuse_scale * inflow - react_scale * absorb[1:-1] * center


def pair_matrix(fine):
    rows = np.arange(fine)[:, None] // 2 == np.arange(fine // 2)[None, :]
    return jnp.asarray(rows.astype(np.float32))


def restrict(field):
    first, second, third = field.shape
    planes = field.reshape(first // 2, 2, second, third).sum(axis=1)
    rows = pair_matrix(second)
    cols = pair_matrix(third)
    out = jnp.einsum("Yy,mYZ,Zz->myz", rows, planes, cols, precision=lax.Precision.HIGHEST)
    return out * 0.125


def prolong(field):
    first, second, third = field.shape
    rows = pair_matrix(second * 2)
    cols = pair_matrix(third * 2)
    out = jnp.einsum("Yy,myz,Zz->mYZ", rows, field, cols, precision=lax.Precision.HIGHEST)
    return jnp.repeat(out, 2, axis=0)


def gather_planes(block, axis_names, pairs_of, distances):
    pieces = {}
    for d in distances:
        if d == 0 and pairs_of(0) is None:
            pieces[d] = block
            continue
        pieces[d] = lax.ppermute(block, axis_names, pairs_of(d))
    return pieces


def shards(initial, guesses, diffusivity, reaction):
    space = lax.axis_size("space")
    times = lax.axis_size("tm")
    me_s = lax.axis_index("space")
    me_t = lax.axis_index("tm")
    n = initial.shape[0]
    halo = STEPS
    reach = -(-halo // n)

    def space_pairs(d):
        return [(s + d, s) for s in range(space) if 0 <= s + d < space]

    def joint(s, t):
        return s * times + t

    def prev_pairs(d):
        return [
            (joint(s + d, (t - 1) % times), joint(s, t))
            for s in range(space)
            for t in range(times)
            if 0 <= s + d < space
        ]

    start = guesses[0]
    distances = [d for d in range(-reach, reach + 1)]
    lo = reach * n - halo
    hi = reach * n + n + halo
    split = times % 2 == 0
    if split:
        even = me_t % 2 == 0
        local = jnp.stack([jnp.where(even, diffusivity, reaction), start])
    else:
        local = jnp.stack([diffusivity, reaction, start])
    got = gather_planes(local, "space", lambda d: None if d == 0 else space_pairs(d), distances)
    wide = jnp.concatenate([got[d] for d in distances], axis=1)
    wide = wide[:, lo:hi]
    if split:
        mine = wide[0]
        rim = jnp.concatenate([mine[:halo], mine[halo + n :]], axis=0)
        partner = [(t, t ^ 1) for t in range(times)]
        theirs_rim = lax.ppermute(rim, "tm", partner)
        theirs_own = jnp.where(even, reaction, diffusivity)
        theirs = jnp.concatenate([theirs_rim[:halo], theirs_own, theirs_rim[halo:]], axis=0)
        conduct = jnp.where(even, mine, theirs)
        absorb = jnp.where(even, theirs, mine)
        field0 = wide[1]
    else:
        conduct, absorb, field0 = wide[0], wide[1], wide[2]
    plane_ids = me_s * n - halo + jnp.arange(n + 2 * halo)
    inside = ((plane_ids >= 0) & (plane_ids < space * n)).astype(jnp.float32)[:, None, None]

    def fine_prop(field):
        for number in range(STEPS):
            cut = number
            k = conduct[cut : conduct.shape[0] - cut]
            c = absorb[cut : absorb.shape[0] - cut]
            field = advance(field, k, c, 0.1, 0.1)
            if number < STEPS - 1:
                m = inside[cut + 1 : inside.shape[0] - cut - 1]
                field = jnp.where(m > 0, field, 0.0)
        return field

    advanced = fine_prop(field0)
    payload = jnp.where(me_t == times - 1, initial, advanced)
    got2 = gather_planes(payload, ("space", "tm"), prev_pairs, distances)
    relaxed = jnp.concatenate([got2[d] for d in distances], axis=0)[lo:hi]
    residual = fine_prop(relaxed) - advanced

    cn = n // 2
    creach = -(-1 // cn)
    cdist = [d for d in range(-creach, creach + 1)]
    coarse_k = restrict(conduct[halo - 2 * creach * cn : halo + n + 2 * creach * cn])
    coarse_c = restrict(absorb[halo - 2 * creach * cn : halo + n + 2 * creach * cn])
    ck = coarse_k[creach * cn - 1 : creach * cn + cn + 1]
    cc = coarse_c[creach * cn - 1 : creach * cn + cn + 1]
    source = restrict(residual)

    def chain_pairs(d):
        return [
            (joint(s + d, t - 1), joint(s, t))
            for s in range(space)
            for t in range(1, times)
            if 0 <= s + d < space
        ]

    partial_error = source
    for turn in range(times - 1):
        got3 = gather_planes(partial_error, ("space", "tm"), chain_pairs, cdist)
        behind = jnp.concatenate([got3[d] for d in cdist], axis=0)
        behind = behind[creach * cn - 1 : creach * cn + cn + 1]
        for number in range(COARSE_STEPS):
            behind = advance(behind, ck, cc, 0.1, 0.4)
        partial_error = source + behind
    corrected = advanced + prolong(partial_error)
    return (corrected[None], residual[None])


def solution(mesh):
    in_specs = (
        P("space", None, None),
        P("tm", "space", None, None),
        P("space", None, None),
        P("space", None, None),
    )
    out_specs = (P("tm", "space", None, None), P("tm", "space", None, None))
    return jax.shard_map(shards, mesh=mesh, in_specs=in_specs, out_specs=out_specs, check_vma=False)
```

```python
import jax
import jax.numpy as jnp
import numpy as np
from jax import lax
from jax.sharding import PartitionSpec as P

STEPS = 4
COARSE_STEPS = STEPS // 4
HALO = 2


def advance(field, conduct, absorb, diffuse_scale, react_scale):
    center = field[1:-1]
    middle = conduct[1:-1]
    padded = jnp.pad(center, ((0, 0), (1, 1), (1, 1)))
    conduct_pad = jnp.pad(middle, ((0, 0), (1, 1), (1, 1)))
    inflow = 0.5 * (conduct[2:] + middle) * (field[2:] - center)
    inflow = inflow + 0.5 * (conduct[:-2] + middle) * (field[:-2] - center)
    inflow = inflow + 0.5 * (conduct_pad[:, 2:, 1:-1] + middle) * (padded[:, 2:, 1:-1] - center)
    inflow = inflow + 0.5 * (conduct_pad[:, :-2, 1:-1] + middle) * (padded[:, :-2, 1:-1] - center)
    inflow = inflow + 0.5 * (conduct_pad[:, 1:-1, 2:] + middle) * (padded[:, 1:-1, 2:] - center)
    inflow = inflow + 0.5 * (conduct_pad[:, 1:-1, :-2] + middle) * (padded[:, 1:-1, :-2] - center)
    return center + diffuse_scale * inflow - react_scale * absorb[1:-1] * center


def pair_matrix(fine):
    rows = np.arange(fine)[:, None] // 2 == np.arange(fine // 2)[None, :]
    return jnp.asarray(rows.astype(np.float32))


def restrict(field):
    first, second, third = field.shape
    planes = field.reshape(first // 2, 2, second, third).sum(axis=1)
    rows = pair_matrix(second)
    cols = pair_matrix(third)
    out = jnp.einsum("Yy,mYZ,Zz->myz", rows, planes, cols, precision=lax.Precision.HIGHEST)
    return out * 0.125


def prolong(field):
    first, second, third = field.shape
    rows = pair_matrix(second * 2)
    cols = pair_matrix(third * 2)
    out = jnp.einsum("Yy,myz,Zz->mYZ", rows, field, cols, precision=lax.Precision.HIGHEST)
    return jnp.repeat(out, 2, axis=0)


def gather_planes(block, axis_names, pairs_of, distances):
    pieces = {}
    for d in distances:
        if d == 0 and pairs_of(0) is None:
            pieces[d] = block
            continue
        pieces[d] = lax.ppermute(block, axis_names, pairs_of(d))
    return pieces


def shards(initial, guesses, diffusivity, reaction):
    space = lax.axis_size("space")
    times = lax.axis_size("tm")
    me_s = lax.axis_index("space")
    me_t = lax.axis_index("tm")
    n = initial.shape[0]
    halo = HALO
    reach = -(-halo // n)
    distances = [d for d in range(-reach, reach + 1)]
    lo = reach * n - halo
    hi = reach * n + n + halo

    def space_pairs(d):
        return [(s + d, s) for s in range(space) if 0 <= s + d < space]

    def joint(s, t):
        return s * times + t

    def prev_pairs(d):
        return [
            (joint(s + d, (t - 1) % times), joint(s, t))
            for s in range(space)
            for t in range(times)
            if 0 <= s + d < space
        ]

    def widen(block, axis):
        got = gather_planes(block, "space", lambda d: None if d == 0 else space_pairs(d), distances)
        wide = jnp.concatenate([got[d] for d in distances], axis=axis)
        return lax.slice_in_dim(wide, lo, hi, axis=axis)

    start = guesses[0]
    split = times % 2 == 0
    if split:
        even = me_t % 2 == 0
        wide = widen(jnp.stack([jnp.where(even, diffusivity, reaction), start]), 1)
        mine = wide[0]
        rim = jnp.concatenate([mine[:halo], mine[halo + n :]], axis=0)
        partner = [(t, t ^ 1) for t in range(times)]
        theirs_rim = lax.ppermute(rim, "tm", partner)
        theirs_own = jnp.where(even, reaction, diffusivity)
        theirs = jnp.concatenate([theirs_rim[:halo], theirs_own, theirs_rim[halo:]], axis=0)
        conduct = jnp.where(even, mine, theirs)
        absorb = jnp.where(even, theirs, mine)
        field0 = wide[1]
    else:
        wide = widen(jnp.stack([diffusivity, reaction, start]), 1)
        conduct, absorb, field0 = wide[0], wide[1], wide[2]
    plane_ids = me_s * n - halo + jnp.arange(n + 2 * halo)
    inside = (plane_ids >= 0) & (plane_ids < space * n)

    def fine_prop(field):
        for number in range(STEPS):
            cut = number % halo
            if number > 0 and cut == 0:
                field = widen(field, 0)
            k = conduct[cut : conduct.shape[0] - cut]
            c = absorb[cut : absorb.shape[0] - cut]
            field = advance(field, k, c, 0.1, 0.1)
            if cut < halo - 1:
                m = inside[cut + 1 : inside.shape[0] - cut - 1][:, None, None]
                field = jnp.where(m, field, 0.0)
        return field

    advanced = fine_prop(field0)
    payload = jnp.where(me_t == times - 1, initial, advanced)
    got2 = gather_planes(payload, ("space", "tm"), prev_pairs, distances)
    relaxed = jnp.concatenate([got2[d] for d in distances], axis=0)[lo:hi]
    residual = fine_prop(relaxed) - advanced

    cn = n // 2
    creach = -(-1 // cn)
    cdist = [d for d in range(-creach, creach + 1)]
    coarse_k = restrict(conduct[halo - 2 * creach * cn : halo + n + 2 * creach * cn])
    coarse_c = restrict(absorb[halo - 2 * creach * cn : halo + n + 2 * creach * cn])
    ck = coarse_k[creach * cn - 1 : creach * cn + cn + 1]
    cc = coarse_c[creach * cn - 1 : creach * cn + cn + 1]
    source = restrict(residual)

    def chain_pairs(d):
        return [
            (joint(s + d, t - 1), joint(s, t))
            for s in range(space)
            for t in range(1, times)
            if 0 <= s + d < space
        ]

    partial_error = source
    for turn in range(times - 1):
        got3 = gather_planes(partial_error, ("space", "tm"), chain_pairs, cdist)
        behind = jnp.concatenate([got3[d] for d in cdist], axis=0)
        behind = behind[creach * cn - 1 : creach * cn + cn + 1]
        for number in range(COARSE_STEPS):
            behind = advance(behind, ck, cc, 0.1, 0.4)
        partial_error = source + behind
    corrected = advanced + prolong(partial_error)
    return (corrected[None], residual[None])


def solution(mesh):
    in_specs = (
        P("space", None, None),
        P("tm", "space", None, None),
        P("space", None, None),
        P("space", None, None),
    )
    out_specs = (P("tm", "space", None, None), P("tm", "space", None, None))
    return jax.shard_map(shards, mesh=mesh, in_specs=in_specs, out_specs=out_specs, check_vma=False)
```

```python
import jax
import jax.numpy as jnp
import numpy as np
from jax import lax
from jax.experimental import pallas as pl
from jax.experimental.pallas import tpu as pltpu
from jax.sharding import PartitionSpec as P
import functools

STEPS = 4
COARSE_STEPS = STEPS // 4
HALO = 4


def advance(field, conduct, absorb, diffuse_scale, react_scale):
    center = field[1:-1]
    middle = conduct[1:-1]
    padded = jnp.pad(center, ((0, 0), (1, 1), (1, 1)))
    conduct_pad = jnp.pad(middle, ((0, 0), (1, 1), (1, 1)))
    inflow = 0.5 * (conduct[2:] + middle) * (field[2:] - center)
    inflow = inflow + 0.5 * (conduct[:-2] + middle) * (field[:-2] - center)
    inflow = inflow + 0.5 * (conduct_pad[:, 2:, 1:-1] + middle) * (padded[:, 2:, 1:-1] - center)
    inflow = inflow + 0.5 * (conduct_pad[:, :-2, 1:-1] + middle) * (padded[:, :-2, 1:-1] - center)
    inflow = inflow + 0.5 * (conduct_pad[:, 1:-1, 2:] + middle) * (padded[:, 1:-1, 2:] - center)
    inflow = inflow + 0.5 * (conduct_pad[:, 1:-1, :-2] + middle) * (padded[:, 1:-1, :-2] - center)
    return center + diffuse_scale * inflow - react_scale * absorb[1:-1] * center


def stencil_plane(vm, v0, vp, km, k0, kp, c0):
    rows, cols = v0.shape
    row = lax.broadcasted_iota(jnp.int32, v0.shape, 0)
    col = lax.broadcasted_iota(jnp.int32, v0.shape, 1)
    top = row < rows - 1
    bottom = row > 0
    right = col < cols - 1
    left = col > 0
    v_yp = jnp.where(top, pltpu.roll(v0, rows - 1, 0), 0.0)
    k_yp = jnp.where(top, pltpu.roll(k0, rows - 1, 0), 0.0)
    v_ym = jnp.where(bottom, pltpu.roll(v0, 1, 0), 0.0)
    k_ym = jnp.where(bottom, pltpu.roll(k0, 1, 0), 0.0)
    v_zp = jnp.where(right, pltpu.roll(v0, cols - 1, 1), 0.0)
    k_zp = jnp.where(right, pltpu.roll(k0, cols - 1, 1), 0.0)
    v_zm = jnp.where(left, pltpu.roll(v0, 1, 1), 0.0)
    k_zm = jnp.where(left, pltpu.roll(k0, 1, 1), 0.0)
    inflow = 0.5 * (kp + k0) * (vp - v0)
    inflow = inflow + 0.5 * (km + k0) * (vm - v0)
    inflow = inflow + 0.5 * (k_yp + k0) * (v_yp - v0)
    inflow = inflow + 0.5 * (k_ym + k0) * (v_ym - v0)
    inflow = inflow + 0.5 * (k_zp + k0) * (v_zp - v0)
    inflow = inflow + 0.5 * (k_zm + k0) * (v_zm - v0)
    return v0 + 0.1 * inflow - 0.1 * c0 * v0


def fine_kernel(steps, meta_ref, f_ref, k_ref, c_ref, o_ref, buf_a, buf_b):
    planes = f_ref.shape[0]
    first = meta_ref[0]
    total = meta_ref[1]
    for step in range(steps):
        src = f_ref if step == 0 else (buf_a if step % 2 == 1 else buf_b)
        last = step == steps - 1
        dst = o_ref if last else (buf_a if step % 2 == 0 else buf_b)
        lo = step + 1
        hi = planes - step - 1

        def body(p, carry, src=src, dst=dst, last=last, lo=lo):
            new = stencil_plane(src[p - 1], src[p], src[p + 1], k_ref[p - 1], k_ref[p], k_ref[p + 1], c_ref[p])
            if last:
                dst[p - lo] = new
            else:
                g = first + p
                ok = (g >= 0) & (g < total)
                dst[p] = jnp.where(ok, new, 0.0)
            return carry

        lax.fori_loop(lo, hi, body, 0)


def fine_prop_kernel(field, conduct, absorb, first, total, steps):
    planes, rows, cols = field.shape
    out_planes = planes - 2 * steps
    meta = jnp.stack([first, total]).astype(jnp.int32)
    cells = rows * cols * sum(planes - 2 * (s + 1) for s in range(steps))
    return pl.pallas_call(
        functools.partial(fine_kernel, steps),
        out_shape=jax.ShapeDtypeStruct((out_planes, rows, cols), jnp.float32),
        in_specs=[pl.BlockSpec(memory_space=pltpu.SMEM)] + [pl.BlockSpec(memory_space=pltpu.VMEM)] * 3,
        out_specs=pl.BlockSpec(memory_space=pltpu.VMEM),
        scratch_shapes=[pltpu.VMEM((planes, rows, cols), jnp.float32)] * 2,
        cost_estimate=pl.CostEstimate(flops=45 * cells, transcendentals=0, bytes_accessed=4 * rows * cols * (3 * planes + out_planes)),
    )(meta, field, conduct, absorb)


def pair_matrix(fine):
    rows = np.arange(fine)[:, None] // 2 == np.arange(fine // 2)[None, :]
    return jnp.asarray(rows.astype(np.float32))


def restrict(field):
    first, second, third = field.shape
    planes = field.reshape(first // 2, 2, second, third).sum(axis=1)
    rows = pair_matrix(second)
    cols = pair_matrix(third)
    out = jnp.einsum("Yy,mYZ,Zz->myz", rows, planes, cols, precision=lax.Precision.HIGHEST)
    return out * 0.125


def prolong(field):
    first, second, third = field.shape
    rows = pair_matrix(second * 2)
    cols = pair_matrix(third * 2)
    out = jnp.einsum("Yy,myz,Zz->mYZ", rows, field, cols, precision=lax.Precision.HIGHEST)
    return jnp.repeat(out, 2, axis=0)


def gather_planes(block, axis_names, pairs_of, distances):
    pieces = {}
    for d in distances:
        if d == 0 and pairs_of(0) is None:
            pieces[d] = block
            continue
        pieces[d] = lax.ppermute(block, axis_names, pairs_of(d))
    return pieces


def shards(initial, guesses, diffusivity, reaction):
    space = lax.axis_size("space")
    times = lax.axis_size("tm")
    me_s = lax.axis_index("space")
    me_t = lax.axis_index("tm")
    n = initial.shape[0]
    halo = HALO
    reach = -(-halo // n)
    distances = [d for d in range(-reach, reach + 1)]
    lo = reach * n - halo
    hi = reach * n + n + halo

    def space_pairs(d):
        return [(s + d, s) for s in range(space) if 0 <= s + d < space]

    def joint(s, t):
        return s * times + t

    def prev_pairs(d):
        return [
            (joint(s + d, (t - 1) % times), joint(s, t))
            for s in range(space)
            for t in range(times)
            if 0 <= s + d < space
        ]

    def widen(block, axis):
        got = gather_planes(block, "space", lambda d: None if d == 0 else space_pairs(d), distances)
        wide = jnp.concatenate([got[d] for d in distances], axis=axis)
        return lax.slice_in_dim(wide, lo, hi, axis=axis)

    start = guesses[0]
    split = times % 2 == 0
    if split:
        even = me_t % 2 == 0
        wide = widen(jnp.stack([jnp.where(even, diffusivity, reaction), start]), 1)
        mine = wide[0]
        rim = jnp.concatenate([mine[:halo], mine[halo + n :]], axis=0)
        partner = [(t, t ^ 1) for t in range(times)]
        theirs_rim = lax.ppermute(rim, "tm", partner)
        theirs_own = jnp.where(even, reaction, diffusivity)
        theirs = jnp.concatenate([theirs_rim[:halo], theirs_own, theirs_rim[halo:]], axis=0)
        conduct = jnp.where(even, mine, theirs)
        absorb = jnp.where(even, theirs, mine)
        field0 = wide[1]
    else:
        wide = widen(jnp.stack([diffusivity, reaction, start]), 1)
        conduct, absorb, field0 = wide[0], wide[1], wide[2]
    plane_ids = me_s * n - halo + jnp.arange(n + 2 * halo)
    inside = (plane_ids >= 0) & (plane_ids < space * n)

    def fine_prop(field):
        if halo == STEPS:
            return fine_prop_kernel(field, conduct, absorb, me_s * n - halo, jnp.int32(space * n), STEPS)
        for number in range(STEPS):
            cut = number % halo
            if number > 0 and cut == 0:
                field = widen(field, 0)
            k = conduct[cut : conduct.shape[0] - cut]
            c = absorb[cut : absorb.shape[0] - cut]
            field = advance(field, k, c, 0.1, 0.1)
            if cut < halo - 1:
                m = inside[cut + 1 : inside.shape[0] - cut - 1][:, None, None]
                field = jnp.where(m, field, 0.0)
        return field

    advanced = fine_prop(field0)
    payload = jnp.where(me_t == times - 1, initial, advanced)
    got2 = gather_planes(payload, ("space", "tm"), prev_pairs, distances)
    relaxed = jnp.concatenate([got2[d] for d in distances], axis=0)[lo:hi]
    residual = fine_prop(relaxed) - advanced

    cn = n // 2
    creach = -(-1 // cn)
    cdist = [d for d in range(-creach, creach + 1)]
    coarse_k = restrict(conduct[halo - 2 * creach * cn : halo + n + 2 * creach * cn])
    coarse_c = restrict(absorb[halo - 2 * creach * cn : halo + n + 2 * creach * cn])
    ck = coarse_k[creach * cn - 1 : creach * cn + cn + 1]
    cc = coarse_c[creach * cn - 1 : creach * cn + cn + 1]
    source = restrict(residual)

    def chain_pairs(d):
        return [
            (joint(s + d, t - 1), joint(s, t))
            for s in range(space)
            for t in range(1, times)
            if 0 <= s + d < space
        ]

    partial_error = source
    for turn in range(times - 1):
        got3 = gather_planes(partial_error, ("space", "tm"), chain_pairs, cdist)
        behind = jnp.concatenate([got3[d] for d in cdist], axis=0)
        behind = behind[creach * cn - 1 : creach * cn + cn + 1]
        for number in range(COARSE_STEPS):
            behind = advance(behind, ck, cc, 0.1, 0.4)
        partial_error = source + behind
    corrected = advanced + prolong(partial_error)
    return (corrected[None], residual[None])


def solution(mesh):
    in_specs = (
        P("space", None, None),
        P("tm", "space", None, None),
        P("space", None, None),
        P("space", None, None),
    )
    out_specs = (P("tm", "space", None, None), P("tm", "space", None, None))
    return jax.shard_map(shards, mesh=mesh, in_specs=in_specs, out_specs=out_specs, check_vma=False)
```

```python
import jax
import jax.numpy as jnp
import numpy as np
from jax import lax
from jax.experimental import pallas as pl
from jax.experimental.pallas import tpu as pltpu
from jax.sharding import PartitionSpec as P
import functools

STEPS = 4
COARSE_STEPS = STEPS // 4
HALO = 4
EDGE = 8
CHUNK = 32


def advance(field, conduct, absorb, diffuse_scale, react_scale):
    center = field[1:-1]
    middle = conduct[1:-1]
    padded = jnp.pad(center, ((0, 0), (1, 1), (1, 1)))
    conduct_pad = jnp.pad(middle, ((0, 0), (1, 1), (1, 1)))
    inflow = 0.5 * (conduct[2:] + middle) * (field[2:] - center)
    inflow = inflow + 0.5 * (conduct[:-2] + middle) * (field[:-2] - center)
    inflow = inflow + 0.5 * (conduct_pad[:, 2:, 1:-1] + middle) * (padded[:, 2:, 1:-1] - center)
    inflow = inflow + 0.5 * (conduct_pad[:, :-2, 1:-1] + middle) * (padded[:, :-2, 1:-1] - center)
    inflow = inflow + 0.5 * (conduct_pad[:, 1:-1, 2:] + middle) * (padded[:, 1:-1, 2:] - center)
    inflow = inflow + 0.5 * (conduct_pad[:, 1:-1, :-2] + middle) * (padded[:, 1:-1, :-2] - center)
    return center + diffuse_scale * inflow - react_scale * absorb[1:-1] * center


def stencil_chunk(vblk, kblk, vm, vp, km, kp, c0):
    size = vblk.shape[0]
    v0 = vblk[EDGE:size - EDGE]
    k0 = kblk[EDGE:size - EDGE]
    v_yp = pltpu.roll(vblk, size - 1, 0)[EDGE:size - EDGE]
    k_yp = pltpu.roll(kblk, size - 1, 0)[EDGE:size - EDGE]
    v_ym = pltpu.roll(vblk, 1, 0)[EDGE:size - EDGE]
    k_ym = pltpu.roll(kblk, 1, 0)[EDGE:size - EDGE]
    cols = v0.shape[1]
    col = lax.broadcasted_iota(jnp.int32, v0.shape, 1)
    right = col < cols - 1
    left = col > 0
    v_zp = jnp.where(right, pltpu.roll(v0, cols - 1, 1), 0.0)
    k_zp = jnp.where(right, pltpu.roll(k0, cols - 1, 1), 0.0)
    v_zm = jnp.where(left, pltpu.roll(v0, 1, 1), 0.0)
    k_zm = jnp.where(left, pltpu.roll(k0, 1, 1), 0.0)
    inflow = 0.5 * (kp + k0) * (vp - v0)
    inflow = inflow + 0.5 * (km + k0) * (vm - v0)
    inflow = inflow + 0.5 * (k_yp + k0) * (v_yp - v0)
    inflow = inflow + 0.5 * (k_ym + k0) * (v_ym - v0)
    inflow = inflow + 0.5 * (k_zp + k0) * (v_zp - v0)
    inflow = inflow + 0.5 * (k_zm + k0) * (v_zm - v0)
    return v0 + 0.1 * inflow - 0.1 * c0 * v0


def fine_kernel(steps, opening, meta_ref, f_ref, mine_ref, theirs_ref, extra_ref, *rest):
    if opening:
        out_ref, send_ref, buf0, buf1, kbuf, cbuf = rest
    else:
        out_ref, buf0, buf1, kbuf, cbuf = rest
    planes, rows, cols = f_ref.shape
    first = meta_ref[0]
    total = meta_ref[1]
    even = meta_ref[2] == 1
    last_interval = meta_ref[3] == 1
    zeros = jnp.zeros((EDGE, cols), jnp.float32)

    def fill(p, carry):
        for buf in (buf0, buf1, kbuf):
            buf[p, pl.ds(0, EDGE), :] = zeros
            buf[p, pl.ds(EDGE + rows, EDGE), :] = zeros
        buf0[p, pl.ds(EDGE, rows), :] = f_ref[p]
        a = mine_ref[p]
        b = theirs_ref[p]
        kbuf[p, pl.ds(EDGE, rows), :] = jnp.where(even, a, b)
        cbuf[p] = jnp.where(even, b, a)
        return carry

    lax.fori_loop(0, planes, fill, 0)
    for step in range(steps):
        src = buf0 if step % 2 == 0 else buf1
        dst = buf1 if step % 2 == 0 else buf0
        final = step == steps - 1
        lo = step + 1
        hi = planes - step - 1

        def body(p, carry, src=src, dst=dst, final=final, lo=lo):
            g = first + p
            ok = (g >= 0) & (g < total)
            for r in range(0, rows, CHUNK):
                base = EDGE + r
                vblk = src[p, pl.ds(base - EDGE, CHUNK + 2 * EDGE), :]
                kblk = kbuf[p, pl.ds(base - EDGE, CHUNK + 2 * EDGE), :]
                vm = src[p - 1, pl.ds(base, CHUNK), :]
                vp = src[p + 1, pl.ds(base, CHUNK), :]
                km = kbuf[p - 1, pl.ds(base, CHUNK), :]
                kp = kbuf[p + 1, pl.ds(base, CHUNK), :]
                c0 = cbuf[p, pl.ds(r, CHUNK), :]
                new = stencil_chunk(vblk, kblk, vm, vp, km, kp, c0)
                if final:
                    q = p - lo
                    ex = extra_ref[q, pl.ds(r, CHUNK), :]
                    if opening:
                        out_ref[q, pl.ds(r, CHUNK), :] = new
                        send_ref[q, pl.ds(r, CHUNK), :] = jnp.where(last_interval, ex, new)
                    else:
                        out_ref[q, pl.ds(r, CHUNK), :] = new - ex
                else:
                    dst[p, pl.ds(base, CHUNK), :] = jnp.where(ok, new, 0.0)
            return carry

        lax.fori_loop(lo, hi, body, 0)


def fine_prop_kernel(field, mine, theirs, extra, meta, steps, opening):
    planes, rows, cols = field.shape
    out_planes = planes - 2 * steps
    cells = rows * cols * sum(planes - 2 * (s + 1) for s in range(steps))
    part = jax.ShapeDtypeStruct((out_planes, rows, cols), jnp.float32)
    vmem = pl.BlockSpec(memory_space=pltpu.VMEM)
    padded = pltpu.VMEM((planes, rows + 2 * EDGE, cols), jnp.float32)
    return pl.pallas_call(
        functools.partial(fine_kernel, steps, opening),
        out_shape=(part, part) if opening else part,
        in_specs=[pl.BlockSpec(memory_space=pltpu.SMEM)] + [vmem] * 4,
        out_specs=(vmem, vmem) if opening else vmem,
        scratch_shapes=[padded, padded, padded, pltpu.VMEM((planes, rows, cols), jnp.float32)],
        cost_estimate=pl.CostEstimate(flops=45 * cells, transcendentals=0, bytes_accessed=4 * rows * cols * (4 * planes + 2 * out_planes)),
    )(meta, field, mine, theirs, extra)


def pair_matrix(fine):
    rows = np.arange(fine)[:, None] // 2 == np.arange(fine // 2)[None, :]
    return jnp.asarray(rows.astype(np.float32))


def restrict(field):
    first, second, third = field.shape
    planes = field.reshape(first // 2, 2, second, third).sum(axis=1)
    rows = pair_matrix(second)
    cols = pair_matrix(third)
    out = jnp.einsum("Yy,mYZ,Zz->myz", rows, planes, cols, precision=lax.Precision.HIGHEST)
    return out * 0.125


def prolong(field):
    first, second, third = field.shape
    rows = pair_matrix(second * 2)
    cols = pair_matrix(third * 2)
    out = jnp.einsum("Yy,myz,Zz->mYZ", rows, field, cols, precision=lax.Precision.HIGHEST)
    return jnp.repeat(out, 2, axis=0)


def gather_planes(block, axis_names, pairs_of, distances):
    pieces = {}
    for d in distances:
        if d == 0 and pairs_of(0) is None:
            pieces[d] = block
            continue
        pieces[d] = lax.ppermute(block, axis_names, pairs_of(d))
    return pieces


def shards(initial, guesses, diffusivity, reaction):
    space = lax.axis_size("space")
    times = lax.axis_size("tm")
    me_s = lax.axis_index("space")
    me_t = lax.axis_index("tm")
    n = initial.shape[0]
    halo = HALO
    reach = -(-halo // n)
    distances = [d for d in range(-reach, reach + 1)]
    lo = reach * n - halo
    hi = reach * n + n + halo

    def space_pairs(d):
        return [(s + d, s) for s in range(space) if 0 <= s + d < space]

    def joint(s, t):
        return s * times + t

    def prev_pairs(d):
        return [
            (joint(s + d, (t - 1) % times), joint(s, t))
            for s in range(space)
            for t in range(times)
            if 0 <= s + d < space
        ]

    def widen(block, axis):
        got = gather_planes(block, "space", lambda d: None if d == 0 else space_pairs(d), distances)
        wide = jnp.concatenate([got[d] for d in distances], axis=axis)
        return lax.slice_in_dim(wide, lo, hi, axis=axis)

    start = guesses[0]
    split = times % 2 == 0
    if split:
        even = me_t % 2 == 0
        wide = widen(jnp.stack([jnp.where(even, diffusivity, reaction), start]), 1)
        mine = wide[0]
        rim = jnp.concatenate([mine[:halo], mine[halo + n :]], axis=0)
        partner = [(t, t ^ 1) for t in range(times)]
        theirs_rim = lax.ppermute(rim, "tm", partner)
        theirs_own = jnp.where(even, reaction, diffusivity)
        theirs = jnp.concatenate([theirs_rim[:halo], theirs_own, theirs_rim[halo:]], axis=0)
        conduct = jnp.where(even, mine, theirs)
        absorb = jnp.where(even, theirs, mine)
        field0 = wide[1]
    else:
        even = True
        wide = widen(jnp.stack([diffusivity, reaction, start]), 1)
        conduct, absorb, field0 = wide[0], wide[1], wide[2]
        mine, theirs = conduct, absorb
    meta = jnp.stack(
        [me_s * n - halo, jnp.int32(space * n), jnp.int32(even), (me_t == times - 1).astype(jnp.int32)]
    ).astype(jnp.int32)
    plane_ids = me_s * n - halo + jnp.arange(n + 2 * halo)
    inside = (plane_ids >= 0) & (plane_ids < space * n)

    def fine_prop(field):
        for number in range(STEPS):
            cut = number % halo
            if number > 0 and cut == 0:
                field = widen(field, 0)
            k = conduct[cut : conduct.shape[0] - cut]
            c = absorb[cut : absorb.shape[0] - cut]
            field = advance(field, k, c, 0.1, 0.1)
            if cut < halo - 1:
                m = inside[cut + 1 : inside.shape[0] - cut - 1][:, None, None]
                field = jnp.where(m, field, 0.0)
        return field

    if halo == STEPS:
        advanced, payload = fine_prop_kernel(field0, mine, theirs, initial, meta, STEPS, True)
    else:
        advanced = fine_prop(field0)
        payload = jnp.where(me_t == times - 1, initial, advanced)
    got2 = gather_planes(payload, ("space", "tm"), prev_pairs, distances)
    relaxed = jnp.concatenate([got2[d] for d in distances], axis=0)[lo:hi]
    if halo == STEPS:
        residual = fine_prop_kernel(relaxed, mine, theirs, advanced, meta, STEPS, False)
    else:
        residual = fine_prop(relaxed) - advanced

    cn = n // 2
    creach = -(-1 // cn)
    cdist = [d for d in range(-creach, creach + 1)]
    coarse_k = restrict(conduct[halo - 2 * creach * cn : halo + n + 2 * creach * cn])
    coarse_c = restrict(absorb[halo - 2 * creach * cn : halo + n + 2 * creach * cn])
    ck = coarse_k[creach * cn - 1 : creach * cn + cn + 1]
    cc = coarse_c[creach * cn - 1 : creach * cn + cn + 1]
    source = restrict(residual)

    def chain_pairs(d):
        return [
            (joint(s + d, t - 1), joint(s, t))
            for s in range(space)
            for t in range(1, times)
            if 0 <= s + d < space
        ]

    partial_error = source
    for turn in range(times - 1):
        got3 = gather_planes(partial_error, ("space", "tm"), chain_pairs, cdist)
        behind = jnp.concatenate([got3[d] for d in cdist], axis=0)
        behind = behind[creach * cn - 1 : creach * cn + cn + 1]
        for number in range(COARSE_STEPS):
            behind = advance(behind, ck, cc, 0.1, 0.4)
        partial_error = source + behind
    corrected = advanced + prolong(partial_error)
    return (corrected[None], residual[None])


def solution(mesh):
    in_specs = (
        P("space", None, None),
        P("tm", "space", None, None),
        P("space", None, None),
        P("space", None, None),
    )
    out_specs = (P("tm", "space", None, None), P("tm", "space", None, None))
    return jax.shard_map(shards, mesh=mesh, in_specs=in_specs, out_specs=out_specs, check_vma=False)
```

```python
import jax
import jax.numpy as jnp
import numpy as np
from jax import lax
from jax.sharding import PartitionSpec as P

STEPS = 4
COARSE_STEPS = STEPS // 4


def advance(field, conduct, absorb, diffuse_scale, react_scale):
    center = field[1:-1]
    middle = conduct[1:-1]
    padded = jnp.pad(center, ((0, 0), (1, 1), (1, 1)))
    conduct_pad = jnp.pad(middle, ((0, 0), (1, 1), (1, 1)))
    inflow = 0.5 * (conduct[2:] + middle) * (field[2:] - center)
    inflow = inflow + 0.5 * (conduct[:-2] + middle) * (field[:-2] - center)
    inflow = inflow + 0.5 * (conduct_pad[:, 2:, 1:-1] + middle) * (padded[:, 2:, 1:-1] - center)
    inflow = inflow + 0.5 * (conduct_pad[:, :-2, 1:-1] + middle) * (padded[:, :-2, 1:-1] - center)
    inflow = inflow + 0.5 * (conduct_pad[:, 1:-1, 2:] + middle) * (padded[:, 1:-1, 2:] - center)
    inflow = inflow + 0.5 * (conduct_pad[:, 1:-1, :-2] + middle) * (padded[:, 1:-1, :-2] - center)
    return center + diffuse_scale * inflow - react_scale * absorb[1:-1] * center


def pair_matrix(fine):
    rows = np.arange(fine)[:, None] // 2 == np.arange(fine // 2)[None, :]
    return jnp.asarray(rows.astype(np.float32))


def restrict(field):
    first, second, third = field.shape
    planes = field.reshape(first // 2, 2, second, third).sum(axis=1)
    rows = pair_matrix(second)
    cols = pair_matrix(third)
    out = jnp.einsum("Yy,mYZ,Zz->myz", rows, planes, cols, precision=lax.Precision.HIGHEST)
    return out * 0.125


def prolong(field):
    first, second, third = field.shape
    rows = pair_matrix(second * 2)
    cols = pair_matrix(third * 2)
    out = jnp.einsum("Yy,myz,Zz->mYZ", rows, field, cols, precision=lax.Precision.HIGHEST)
    return jnp.repeat(out, 2, axis=0)


def gather_planes(block, axis_names, pairs_of, distances):
    pieces = {}
    for d in distances:
        if d == 0 and pairs_of(0) is None:
            pieces[d] = block
            continue
        pieces[d] = lax.ppermute(block, axis_names, pairs_of(d))
    return pieces


def shards(initial, guesses, diffusivity, reaction):
    space = lax.axis_size("space")
    times = lax.axis_size("tm")
    me_s = lax.axis_index("space")
    me_t = lax.axis_index("tm")
    n = initial.shape[0]
    halo = STEPS
    reach = -(-halo // n)

    def space_pairs(d):
        return [(s + d, s) for s in range(space) if 0 <= s + d < space]

    def joint(s, t):
        return s * times + t

    def prev_pairs(d):
        return [
            (joint(s + d, (t - 1) % times), joint(s, t))
            for s in range(space)
            for t in range(times)
            if 0 <= s + d < space
        ]

    start = guesses[0]
    distances = [d for d in range(-reach, reach + 1)]
    lo = reach * n - halo
    hi = reach * n + n + halo
    split = times % 2 == 0
    if split:
        even = me_t % 2 == 0
        local = jnp.where(even, jnp.stack([diffusivity, start]), jnp.stack([reaction, start]))
    else:
        local = jnp.stack([diffusivity, reaction, start])
    got = gather_planes(local, "space", lambda d: None if d == 0 else space_pairs(d), distances)
    wide = jnp.concatenate([got[d] for d in distances], axis=1)
    wide = wide[:, lo:hi]
    if split:
        mine = wide[0]
        rim = jnp.concatenate([mine[:halo], mine[halo + n :]], axis=0)
        partner = [(t, t ^ 1) for t in range(times)]
        theirs_rim = lax.ppermute(rim, "tm", partner)
        theirs_own = jnp.where(even, reaction, diffusivity)
        theirs = jnp.concatenate([theirs_rim[:halo], theirs_own, theirs_rim[halo:]], axis=0)
        conduct = jnp.where(even, mine, theirs)
        absorb = jnp.where(even, theirs, mine)
        field0 = wide[1]
    else:
        conduct, absorb, field0 = wide[0], wide[1], wide[2]
    plane_ids = me_s * n - halo + jnp.arange(n + 2 * halo)
    inside = ((plane_ids >= 0) & (plane_ids < space * n)).astype(jnp.float32)[:, None, None]

    def fine_prop(field):
        for number in range(STEPS):
            cut = number
            k = conduct[cut : conduct.shape[0] - cut]
            c = absorb[cut : absorb.shape[0] - cut]
            field = advance(field, k, c, 0.1, 0.1)
            if number < STEPS - 1:
                m = inside[cut + 1 : inside.shape[0] - cut - 1]
                field = jnp.where(m > 0, field, 0.0)
        return field

    advanced = fine_prop(field0)
    payload = jnp.where(me_t == times - 1, initial, advanced)
    got2 = gather_planes(payload, ("space", "tm"), prev_pairs, distances)
    relaxed = jnp.concatenate([got2[d] for d in distances], axis=0)[lo:hi]
    residual = fine_prop(relaxed) - advanced

    cn = n // 2
    creach = -(-1 // cn)
    cdist = [d for d in range(-creach, creach + 1)]
    coarse_k = restrict(conduct[halo - 2 * creach * cn : halo + n + 2 * creach * cn])
    coarse_c = restrict(absorb[halo - 2 * creach * cn : halo + n + 2 * creach * cn])
    ck = coarse_k[creach * cn - 1 : creach * cn + cn + 1]
    cc = coarse_c[creach * cn - 1 : creach * cn + cn + 1]
    source = restrict(residual)

    def chain_pairs(d):
        return [
            (joint(s + d, t - 1), joint(s, t))
            for s in range(space)
            for t in range(1, times)
            if 0 <= s + d < space
        ]

    partial_error = source
    for turn in range(times - 1):
        got3 = gather_planes(partial_error, ("space", "tm"), chain_pairs, cdist)
        behind = jnp.concatenate([got3[d] for d in cdist], axis=0)
        behind = behind[creach * cn - 1 : creach * cn + cn + 1]
        for number in range(COARSE_STEPS):
            behind = advance(behind, ck, cc, 0.1, 0.4)
        partial_error = source + behind
    corrected = advanced + prolong(partial_error)
    return (corrected[None], residual[None])


def solution(mesh):
    in_specs = (
        P("space", None, None),
        P("tm", "space", None, None),
        P("space", None, None),
        P("space", None, None),
    )
    out_specs = (P("tm", "space", None, None), P("tm", "space", None, None))
    return jax.shard_map(shards, mesh=mesh, in_specs=in_specs, out_specs=out_specs, check_vma=False)
```

```python
import jax
import jax.numpy as jnp
import numpy as np
from jax import lax
from jax.sharding import PartitionSpec as P

STEPS = 4
COARSE_STEPS = STEPS // 4


def advance(field, conduct, absorb, diffuse_scale, react_scale):
    center = field[1:-1]
    middle = conduct[1:-1]
    padded = jnp.pad(center, ((0, 0), (1, 1), (1, 1)))
    conduct_pad = jnp.pad(middle, ((0, 0), (1, 1), (1, 1)))
    inflow = 0.5 * (conduct[2:] + middle) * (field[2:] - center)
    inflow = inflow + 0.5 * (conduct[:-2] + middle) * (field[:-2] - center)
    inflow = inflow + 0.5 * (conduct_pad[:, 2:, 1:-1] + middle) * (padded[:, 2:, 1:-1] - center)
    inflow = inflow + 0.5 * (conduct_pad[:, :-2, 1:-1] + middle) * (padded[:, :-2, 1:-1] - center)
    inflow = inflow + 0.5 * (conduct_pad[:, 1:-1, 2:] + middle) * (padded[:, 1:-1, 2:] - center)
    inflow = inflow + 0.5 * (conduct_pad[:, 1:-1, :-2] + middle) * (padded[:, 1:-1, :-2] - center)
    return center + diffuse_scale * inflow - react_scale * absorb[1:-1] * center


def pair_matrix(fine):
    rows = np.arange(fine)[:, None] // 2 == np.arange(fine // 2)[None, :]
    return jnp.asarray(rows.astype(np.float32))


def restrict(field):
    first, second, third = field.shape
    planes = field.reshape(first // 2, 2, second, third).sum(axis=1)
    rows = pair_matrix(second)
    cols = pair_matrix(third)
    out = jnp.einsum("Yy,mYZ,Zz->myz", rows, planes, cols, precision=lax.Precision.HIGHEST)
    return out * 0.125


def prolong(field):
    first, second, third = field.shape
    rows = pair_matrix(second * 2)
    cols = pair_matrix(third * 2)
    out = jnp.einsum("Yy,myz,Zz->mYZ", rows, field, cols, precision=lax.Precision.HIGHEST)
    return jnp.repeat(out, 2, axis=0)


def gather_planes(block, axis_names, pairs_of, distances):
    pieces = {}
    for d in distances:
        if d == 0 and pairs_of(0) is None:
            pieces[d] = block
            continue
        pieces[d] = lax.ppermute(block, axis_names, pairs_of(d))
    return pieces


def shards(initial, guesses, diffusivity, reaction):
    space = lax.axis_size("space")
    times = lax.axis_size("tm")
    me_s = lax.axis_index("space")
    me_t = lax.axis_index("tm")
    n = initial.shape[0]
    halo = STEPS
    reach = -(-halo // n)

    def space_pairs(d):
        return [(s + d, s) for s in range(space) if 0 <= s + d < space]

    def joint(s, t):
        return s * times + t

    def prev_pairs(d):
        return [
            (joint(s + d, t - 1), joint(s, t))
            for s in range(space)
            for t in range(1, times)
            if 0 <= s + d < space
        ]

    def chain_pairs(d):
        return [
            (joint(s + d, t - 1), joint(s, t))
            for s in range(space)
            for t in range(1, times)
            if 0 <= s + d < space
        ]

    def first_pairs(d):
        if d == 0:
            return None
        return [(joint(s + d, times - 1), joint(s, 0)) for s in range(space) if 0 <= s + d < space]

    cn = n // 2
    creach = -(-1 // cn)
    cdist = [d for d in range(-creach, creach + 1)]
    start = guesses[0]
    distances = [d for d in range(-reach, reach + 1)]
    lo = reach * n - halo
    hi = reach * n + n + halo
    split = times % 2 == 0
    if split:
        even = me_t % 2 == 0
        local = jnp.where(even, jnp.stack([diffusivity, start]), jnp.stack([reaction, start]))
    else:
        local = jnp.stack([diffusivity, reaction, start])
    got = gather_planes(local, "space", lambda d: None if d == 0 else space_pairs(d), distances)
    wide = jnp.concatenate([got[d] for d in distances], axis=1)
    wide = wide[:, lo:hi]
    if split:
        mine = wide[0]
        rim = jnp.concatenate([mine[:halo], mine[halo + n :]], axis=0)
        partner = [(t, t ^ 1) for t in range(times)]
        theirs_rim = lax.ppermute(rim, "tm", partner)
        theirs_own = jnp.where(even, reaction, diffusivity)
        theirs = jnp.concatenate([theirs_rim[:halo], theirs_own, theirs_rim[halo:]], axis=0)
        conduct = jnp.where(even, mine, theirs)
        absorb = jnp.where(even, theirs, mine)
        field0 = wide[1]
    else:
        conduct, absorb, field0 = wide[0], wide[1], wide[2]
    plane_ids = me_s * n - halo + jnp.arange(n + 2 * halo)
    inside = ((plane_ids >= 0) & (plane_ids < space * n)).astype(jnp.float32)[:, None, None]

    def fine_prop(field):
        for number in range(STEPS):
            cut = number
            k = conduct[cut : conduct.shape[0] - cut]
            c = absorb[cut : absorb.shape[0] - cut]
            field = advance(field, k, c, 0.1, 0.1)
            if number < STEPS - 1:
                m = inside[cut + 1 : inside.shape[0] - cut - 1]
                field = jnp.where(m > 0, field, 0.0)
        return field

    got1 = gather_planes(initial, ("space", "tm"), first_pairs, distances)
    opening = jnp.concatenate([got1[d] for d in distances], axis=0)[lo:hi]
    advanced = fine_prop(field0)
    got2 = gather_planes(advanced, ("space", "tm"), prev_pairs, distances)
    behind = jnp.concatenate([got2[d] for d in distances], axis=0)[lo:hi]
    early = fine_prop(opening) - advanced
    early_source = restrict(early)
    sent_early = None
    if times == 2:
        sent_early = gather_planes(early_source, ("space", "tm"), chain_pairs, cdist)
        behind, sent_early = lax.optimization_barrier((behind, sent_early))
    late = fine_prop(behind) - advanced
    first = me_t == 0
    residual = jnp.where(first, early, late)

    coarse_k = restrict(conduct[halo - 2 * creach * cn : halo + n + 2 * creach * cn])
    coarse_c = restrict(absorb[halo - 2 * creach * cn : halo + n + 2 * creach * cn])
    ck = coarse_k[creach * cn - 1 : creach * cn + cn + 1]
    cc = coarse_c[creach * cn - 1 : creach * cn + cn + 1]
    source = jnp.where(first, early_source, restrict(late))

    partial_error = source
    for turn in range(times - 1):
        got3 = sent_early if sent_early is not None else gather_planes(partial_error, ("space", "tm"), chain_pairs, cdist)
        behind = jnp.concatenate([got3[d] for d in cdist], axis=0)
        behind = behind[creach * cn - 1 : creach * cn + cn + 1]
        for number in range(COARSE_STEPS):
            behind = advance(behind, ck, cc, 0.1, 0.4)
        partial_error = source + behind
    corrected = advanced + prolong(partial_error)
    return (corrected[None], residual[None])


def solution(mesh):
    in_specs = (
        P("space", None, None),
        P("tm", "space", None, None),
        P("space", None, None),
        P("space", None, None),
    )
    out_specs = (P("tm", "space", None, None), P("tm", "space", None, None))
    return jax.shard_map(shards, mesh=mesh, in_specs=in_specs, out_specs=out_specs, check_vma=False)
```

```python
import jax
import jax.numpy as jnp
import numpy as np
from jax import lax
from jax.sharding import PartitionSpec as P

STEPS = 4
COARSE_STEPS = STEPS // 4


def advance(field, conduct, absorb, diffuse_scale, react_scale):
    center = field[1:-1]
    middle = conduct[1:-1]
    padded = jnp.pad(center, ((0, 0), (1, 1), (1, 1)))
    conduct_pad = jnp.pad(middle, ((0, 0), (1, 1), (1, 1)))
    inflow = 0.5 * (conduct[2:] + middle) * (field[2:] - center)
    inflow = inflow + 0.5 * (conduct[:-2] + middle) * (field[:-2] - center)
    inflow = inflow + 0.5 * (conduct_pad[:, 2:, 1:-1] + middle) * (padded[:, 2:, 1:-1] - center)
    inflow = inflow + 0.5 * (conduct_pad[:, :-2, 1:-1] + middle) * (padded[:, :-2, 1:-1] - center)
    inflow = inflow + 0.5 * (conduct_pad[:, 1:-1, 2:] + middle) * (padded[:, 1:-1, 2:] - center)
    inflow = inflow + 0.5 * (conduct_pad[:, 1:-1, :-2] + middle) * (padded[:, 1:-1, :-2] - center)
    return center + diffuse_scale * inflow - react_scale * absorb[1:-1] * center


def pair_matrix(fine):
    rows = np.arange(fine)[:, None] // 2 == np.arange(fine // 2)[None, :]
    return jnp.asarray(rows.astype(np.float32))


def restrict(field):
    first, second, third = field.shape
    planes = field.reshape(first // 2, 2, second, third).sum(axis=1)
    rows = pair_matrix(second)
    cols = pair_matrix(third)
    out = jnp.einsum("Yy,mYZ,Zz->myz", rows, planes, cols, precision=lax.Precision.HIGHEST)
    return out * 0.125


def prolong(field):
    first, second, third = field.shape
    rows = pair_matrix(second * 2)
    cols = pair_matrix(third * 2)
    out = jnp.einsum("Yy,myz,Zz->mYZ", rows, field, cols, precision=lax.Precision.HIGHEST)
    return jnp.repeat(out, 2, axis=0)


def gather_planes(block, axis_names, pairs_of, distances):
    pieces = {}
    for d in distances:
        if d == 0 and pairs_of(0) is None:
            pieces[d] = block
            continue
        pieces[d] = lax.ppermute(block, axis_names, pairs_of(d))
    return pieces


def shards(initial, guesses, diffusivity, reaction):
    space = lax.axis_size("space")
    times = lax.axis_size("tm")
    me_s = lax.axis_index("space")
    me_t = lax.axis_index("tm")
    n = initial.shape[0]
    halo = STEPS
    reach = -(-halo // n)

    def space_pairs(d):
        return [(s + d, s) for s in range(space) if 0 <= s + d < space]

    def joint(s, t):
        return s * times + t

    def prev_pairs(d):
        return [
            (joint(s + d, (t - 1) % times), joint(s, t))
            for s in range(space)
            for t in range(times)
            if 0 <= s + d < space
        ]

    start = guesses[0]
    distances = [d for d in range(-reach, reach + 1)]
    lo = reach * n - halo
    hi = reach * n + n + halo
    split = times % 2 == 0
    if split:
        even = me_t % 2 == 0
        local = jnp.where(even, jnp.stack([diffusivity, start]), jnp.stack([reaction, start]))
    else:
        local = jnp.stack([diffusivity, reaction, start])
    got = gather_planes(local, "space", lambda d: None if d == 0 else space_pairs(d), distances)
    wide = jnp.concatenate([got[d] for d in distances], axis=1)
    wide = wide[:, lo:hi]
    if split:
        mine = wide[0]
        rim = jnp.concatenate([mine[:halo], mine[halo + n :]], axis=0)
        partner = [(t, t ^ 1) for t in range(times)]
        theirs_rim = lax.ppermute(rim, "tm", partner)
        theirs_own = jnp.where(even, reaction, diffusivity)
        theirs = jnp.concatenate([theirs_rim[:halo], theirs_own, theirs_rim[halo:]], axis=0)
        conduct = jnp.where(even, mine, theirs)
        absorb = jnp.where(even, theirs, mine)
        field0 = wide[1]
    else:
        conduct, absorb, field0 = wide[0], wide[1], wide[2]
    plane_ids = me_s * n - halo + jnp.arange(n + 2 * halo)
    inside = ((plane_ids >= 0) & (plane_ids < space * n)).astype(jnp.float32)[:, None, None]

    def fine_prop(field):
        for number in range(STEPS):
            cut = number
            k = conduct[cut : conduct.shape[0] - cut]
            c = absorb[cut : absorb.shape[0] - cut]
            field = advance(field, k, c, 0.1, 0.1)
            if number < STEPS - 1:
                m = inside[cut + 1 : inside.shape[0] - cut - 1]
                field = jnp.where(m > 0, field, 0.0)
        return field

    advanced = fine_prop(field0)
    payload = lax.cond(me_t == times - 1, lambda: initial, lambda: advanced)
    got2 = gather_planes(payload, ("space", "tm"), prev_pairs, distances)
    relaxed = jnp.concatenate([got2[d] for d in distances], axis=0)[lo:hi]
    residual = fine_prop(relaxed) - advanced

    cn = n // 2
    creach = -(-1 // cn)
    cdist = [d for d in range(-creach, creach + 1)]
    coarse_k = restrict(conduct[halo - 2 * creach * cn : halo + n + 2 * creach * cn])
    coarse_c = restrict(absorb[halo - 2 * creach * cn : halo + n + 2 * creach * cn])
    ck = coarse_k[creach * cn - 1 : creach * cn + cn + 1]
    cc = coarse_c[creach * cn - 1 : creach * cn + cn + 1]
    source = restrict(residual)

    def chain_pairs(d):
        return [
            (joint(s + d, t - 1), joint(s, t))
            for s in range(space)
            for t in range(1, times)
            if 0 <= s + d < space
        ]

    partial_error = source
    for turn in range(times - 1):
        got3 = gather_planes(partial_error, ("space", "tm"), chain_pairs, cdist)
        behind = jnp.concatenate([got3[d] for d in cdist], axis=0)
        behind = behind[creach * cn - 1 : creach * cn + cn + 1]
        for number in range(COARSE_STEPS):
            behind = advance(behind, ck, cc, 0.1, 0.4)
        partial_error = source + behind
    corrected = advanced + prolong(partial_error)
    return (corrected[None], residual[None])


def solution(mesh):
    in_specs = (
        P("space", None, None),
        P("tm", "space", None, None),
        P("space", None, None),
        P("space", None, None),
    )
    out_specs = (P("tm", "space", None, None), P("tm", "space", None, None))
    return jax.shard_map(shards, mesh=mesh, in_specs=in_specs, out_specs=out_specs, check_vma=False)
```

```python
import jax
import jax.numpy as jnp
import numpy as np
from jax import lax
from jax.sharding import PartitionSpec as P

STEPS = 4
COARSE_STEPS = STEPS // 4


def advance(field, conduct, absorb, diffuse_scale, react_scale):
    center = field[1:-1]
    middle = conduct[1:-1]
    padded = jnp.pad(center, ((0, 0), (1, 1), (1, 1)))
    conduct_pad = jnp.pad(middle, ((0, 0), (1, 1), (1, 1)))
    inflow = 0.5 * (conduct[2:] + middle) * (field[2:] - center)
    inflow = inflow + 0.5 * (conduct[:-2] + middle) * (field[:-2] - center)
    inflow = inflow + 0.5 * (conduct_pad[:, 2:, 1:-1] + middle) * (padded[:, 2:, 1:-1] - center)
    inflow = inflow + 0.5 * (conduct_pad[:, :-2, 1:-1] + middle) * (padded[:, :-2, 1:-1] - center)
    inflow = inflow + 0.5 * (conduct_pad[:, 1:-1, 2:] + middle) * (padded[:, 1:-1, 2:] - center)
    inflow = inflow + 0.5 * (conduct_pad[:, 1:-1, :-2] + middle) * (padded[:, 1:-1, :-2] - center)
    return center + diffuse_scale * inflow - react_scale * absorb[1:-1] * center


def pair_matrix(fine):
    rows = np.arange(fine)[:, None] // 2 == np.arange(fine // 2)[None, :]
    return jnp.asarray(rows.astype(np.float32))


def restrict(field):
    first, second, third = field.shape
    planes = field.reshape(first // 2, 2, second, third).sum(axis=1)
    rows = pair_matrix(second)
    cols = pair_matrix(third)
    out = jnp.einsum("Yy,mYZ,Zz->myz", rows, planes, cols, precision=lax.Precision.HIGHEST)
    return out * 0.125


def prolong(field):
    first, second, third = field.shape
    rows = pair_matrix(second * 2)
    cols = pair_matrix(third * 2)
    out = jnp.einsum("Yy,myz,Zz->mYZ", rows, field, cols, precision=lax.Precision.HIGHEST)
    return jnp.repeat(out, 2, axis=0)


def gather_planes(block, axis_names, pairs_of, distances):
    pieces = {}
    for d in distances:
        if d == 0 and pairs_of(0) is None:
            pieces[d] = block
            continue
        pieces[d] = lax.ppermute(block, axis_names, pairs_of(d))
    return pieces


def shards(initial, guesses, diffusivity, reaction):
    space = lax.axis_size("space")
    times = lax.axis_size("tm")
    me_s = lax.axis_index("space")
    me_t = lax.axis_index("tm")
    n = initial.shape[0]
    halo = STEPS
    reach = -(-halo // n)

    def space_pairs(d):
        return [(s + d, s) for s in range(space) if 0 <= s + d < space]

    def joint(s, t):
        return s * times + t

    def prev_pairs(d):
        return [
            (joint(s + d, (t - 1) % times), joint(s, t))
            for s in range(space)
            for t in range(times)
            if 0 <= s + d < space
        ]

    start = guesses[0]
    distances = [d for d in range(-reach, reach + 1)]
    lo = reach * n - halo
    hi = reach * n + n + halo
    split = times % 2 == 0
    if split:
        even = me_t % 2 == 0
        partner = [(t, t ^ 1) for t in range(times)]
        other = lax.ppermute(start, "tm", partner)
        local = jnp.where(
            even,
            jnp.stack([start, other, diffusivity, reaction]),
            jnp.stack([other, start, diffusivity, reaction]),
        )

        def side_pairs(d):
            pairs = []
            for s in range(space):
                for t in range(times):
                    src_s = s - d if t % 2 == 0 else s + d
                    if 0 <= src_s < space:
                        pairs.append((joint(src_s, t), joint(s, t)))
            return pairs

        near = [lax.ppermute(local, ("space", "tm"), side_pairs(d)) for d in range(1, reach + 1)]
        keep = jnp.where(
            even,
            jnp.stack([jnp.stack([blk[1], blk[2], blk[3]]) for blk in near]),
            jnp.stack([jnp.stack([blk[0], blk[2], blk[3]]) for blk in near]),
        )
        handed = lax.ppermute(keep, "tm", partner)
        own_g = jnp.where(even, jnp.stack([blk[0] for blk in near]), jnp.stack([blk[1] for blk in near]))
        own_kc = jnp.stack([jnp.stack([blk[2], blk[3]]) for blk in near])
        here = jnp.concatenate([own_g[:, None], own_kc], axis=1)
        left = jnp.where(even, here, handed)
        right = jnp.where(even, handed, here)
        centre = jnp.stack([start, diffusivity, reaction])
        pieces = [left[reach - 1 - i] for i in range(reach)] + [centre] + [right[i] for i in range(reach)]
        wide = jnp.concatenate(pieces, axis=1)[:, lo:hi]
        field0, conduct, absorb = wide[0], wide[1], wide[2]
    else:
        local = jnp.stack([diffusivity, reaction, start])
        got = gather_planes(local, "space", lambda d: None if d == 0 else space_pairs(d), distances)
        wide = jnp.concatenate([got[d] for d in distances], axis=1)[:, lo:hi]
        conduct, absorb, field0 = wide[0], wide[1], wide[2]
    plane_ids = me_s * n - halo + jnp.arange(n + 2 * halo)
    inside = ((plane_ids >= 0) & (plane_ids < space * n)).astype(jnp.float32)[:, None, None]

    def fine_prop(field):
        for number in range(STEPS):
            cut = number
            k = conduct[cut : conduct.shape[0] - cut]
            c = absorb[cut : absorb.shape[0] - cut]
            field = advance(field, k, c, 0.1, 0.1)
            if number < STEPS - 1:
                m = inside[cut + 1 : inside.shape[0] - cut - 1]
                field = jnp.where(m > 0, field, 0.0)
        return field

    advanced = fine_prop(field0)
    payload = jnp.where(me_t == times - 1, initial, advanced)
    got2 = gather_planes(payload, ("space", "tm"), prev_pairs, distances)
    relaxed = jnp.concatenate([got2[d] for d in distances], axis=0)[lo:hi]
    residual = fine_prop(relaxed) - advanced

    cn = n // 2
    creach = -(-1 // cn)
    cdist = [d for d in range(-creach, creach + 1)]
    coarse_k = restrict(conduct[halo - 2 * creach * cn : halo + n + 2 * creach * cn])
    coarse_c = restrict(absorb[halo - 2 * creach * cn : halo + n + 2 * creach * cn])
    ck = coarse_k[creach * cn - 1 : creach * cn + cn + 1]
    cc = coarse_c[creach * cn - 1 : creach * cn + cn + 1]
    source = restrict(residual)

    def chain_pairs(d):
        return [
            (joint(s + d, t - 1), joint(s, t))
            for s in range(space)
            for t in range(1, times)
            if 0 <= s + d < space
        ]

    partial_error = source
    for turn in range(times - 1):
        got3 = gather_planes(partial_error, ("space", "tm"), chain_pairs, cdist)
        behind = jnp.concatenate([got3[d] for d in cdist], axis=0)
        behind = behind[creach * cn - 1 : creach * cn + cn + 1]
        for number in range(COARSE_STEPS):
            behind = advance(behind, ck, cc, 0.1, 0.4)
        partial_error = source + behind
    corrected = advanced + prolong(partial_error)
    return (corrected[None], residual[None])


def solution(mesh):
    in_specs = (
        P("space", None, None),
        P("tm", "space", None, None),
        P("space", None, None),
        P("space", None, None),
    )
    out_specs = (P("tm", "space", None, None), P("tm", "space", None, None))
    return jax.shard_map(shards, mesh=mesh, in_specs=in_specs, out_specs=out_specs, check_vma=False)
```

```python
import jax
import jax.numpy as jnp
import numpy as np
from jax import lax
from jax.sharding import PartitionSpec as P

STEPS = 4
COARSE_STEPS = STEPS // 4


def advance(field, conduct, absorb, diffuse_scale, react_scale):
    center = field[1:-1]
    middle = conduct[1:-1]
    padded = jnp.pad(center, ((0, 0), (1, 1), (1, 1)))
    conduct_pad = jnp.pad(middle, ((0, 0), (1, 1), (1, 1)))
    inflow = 0.5 * (conduct[2:] + middle) * (field[2:] - center)
    inflow = inflow + 0.5 * (conduct[:-2] + middle) * (field[:-2] - center)
    inflow = inflow + 0.5 * (conduct_pad[:, 2:, 1:-1] + middle) * (padded[:, 2:, 1:-1] - center)
    inflow = inflow + 0.5 * (conduct_pad[:, :-2, 1:-1] + middle) * (padded[:, :-2, 1:-1] - center)
    inflow = inflow + 0.5 * (conduct_pad[:, 1:-1, 2:] + middle) * (padded[:, 1:-1, 2:] - center)
    inflow = inflow + 0.5 * (conduct_pad[:, 1:-1, :-2] + middle) * (padded[:, 1:-1, :-2] - center)
    return center + diffuse_scale * inflow - react_scale * absorb[1:-1] * center


def pair_matrix(fine):
    rows = np.arange(fine)[:, None] // 2 == np.arange(fine // 2)[None, :]
    return jnp.asarray(rows.astype(np.float32))


def restrict(field):
    first, second, third = field.shape
    planes = field.reshape(first // 2, 2, second, third).sum(axis=1)
    rows = pair_matrix(second)
    cols = pair_matrix(third)
    out = jnp.einsum("Yy,mYZ,Zz->myz", rows, planes, cols, precision=lax.Precision.HIGH)
    return out * 0.125


def prolong(field):
    first, second, third = field.shape
    rows = pair_matrix(second * 2)
    cols = pair_matrix(third * 2)
    out = jnp.einsum("Yy,myz,Zz->mYZ", rows, field, cols, precision=lax.Precision.HIGH)
    return jnp.repeat(out, 2, axis=0)


def gather_planes(block, axis_names, pairs_of, distances):
    pieces = {}
    for d in distances:
        if d == 0 and pairs_of(0) is None:
            pieces[d] = block
            continue
        pieces[d] = lax.ppermute(block, axis_names, pairs_of(d))
    return pieces


def shards(initial, guesses, diffusivity, reaction):
    space = lax.axis_size("space")
    times = lax.axis_size("tm")
    me_s = lax.axis_index("space")
    me_t = lax.axis_index("tm")
    n = initial.shape[0]
    halo = STEPS
    reach = -(-halo // n)

    def space_pairs(d):
        return [(s + d, s) for s in range(space) if 0 <= s + d < space]

    def joint(s, t):
        return s * times + t

    def prev_pairs(d):
        return [
            (joint(s + d, (t - 1) % times), joint(s, t))
            for s in range(space)
            for t in range(times)
            if 0 <= s + d < space
        ]

    start = guesses[0]
    distances = [d for d in range(-reach, reach + 1)]
    lo = reach * n - halo
    hi = reach * n + n + halo
    split = times % 2 == 0
    if split:
        even = me_t % 2 == 0
        local = jnp.where(even, jnp.stack([diffusivity, start]), jnp.stack([reaction, start]))
    else:
        local = jnp.stack([diffusivity, reaction, start])
    got = gather_planes(local, "space", lambda d: None if d == 0 else space_pairs(d), distances)
    wide = jnp.concatenate([got[d] for d in distances], axis=1)
    wide = wide[:, lo:hi]
    if split:
        mine = wide[0]
        rim = jnp.concatenate([mine[:halo], mine[halo + n :]], axis=0)
        partner = [(t, t ^ 1) for t in range(times)]
        theirs_rim = lax.ppermute(rim, "tm", partner)
        theirs_own = jnp.where(even, reaction, diffusivity)
        theirs = jnp.concatenate([theirs_rim[:halo], theirs_own, theirs_rim[halo:]], axis=0)
        conduct = jnp.where(even, mine, theirs)
        absorb = jnp.where(even, theirs, mine)
        field0 = wide[1]
    else:
        conduct, absorb, field0 = wide[0], wide[1], wide[2]
    plane_ids = me_s * n - halo + jnp.arange(n + 2 * halo)
    inside = ((plane_ids >= 0) & (plane_ids < space * n)).astype(jnp.float32)[:, None, None]

    def fine_prop(field):
        for number in range(STEPS):
            cut = number
            k = conduct[cut : conduct.shape[0] - cut]
            c = absorb[cut : absorb.shape[0] - cut]
            field = advance(field, k, c, 0.1, 0.1)
            if number < STEPS - 1:
                m = inside[cut + 1 : inside.shape[0] - cut - 1]
                field = jnp.where(m > 0, field, 0.0)
        return field

    advanced = fine_prop(field0)
    payload = jnp.where(me_t == times - 1, initial, advanced)
    got2 = gather_planes(payload, ("space", "tm"), prev_pairs, distances)
    relaxed = jnp.concatenate([got2[d] for d in distances], axis=0)[lo:hi]
    residual = fine_prop(relaxed) - advanced

    cn = n // 2
    creach = -(-1 // cn)
    cdist = [d for d in range(-creach, creach + 1)]
    coarse_k = restrict(conduct[halo - 2 * creach * cn : halo + n + 2 * creach * cn])
    coarse_c = restrict(absorb[halo - 2 * creach * cn : halo + n + 2 * creach * cn])
    ck = coarse_k[creach * cn - 1 : creach * cn + cn + 1]
    cc = coarse_c[creach * cn - 1 : creach * cn + cn + 1]
    source = restrict(residual)

    def chain_pairs(d):
        return [
            (joint(s + d, t - 1), joint(s, t))
            for s in range(space)
            for t in range(1, times)
            if 0 <= s + d < space
        ]

    partial_error = source
    for turn in range(times - 1):
        got3 = gather_planes(partial_error, ("space", "tm"), chain_pairs, cdist)
        behind = jnp.concatenate([got3[d] for d in cdist], axis=0)
        behind = behind[creach * cn - 1 : creach * cn + cn + 1]
        for number in range(COARSE_STEPS):
            behind = advance(behind, ck, cc, 0.1, 0.4)
        partial_error = source + behind
    corrected = advanced + prolong(partial_error)
    return (corrected[None], residual[None])


def solution(mesh):
    in_specs = (
        P("space", None, None),
        P("tm", "space", None, None),
        P("space", None, None),
        P("space", None, None),
    )
    out_specs = (P("tm", "space", None, None), P("tm", "space", None, None))
    return jax.shard_map(shards, mesh=mesh, in_specs=in_specs, out_specs=out_specs, check_vma=False)
```

```python
import jax
import jax.numpy as jnp
import numpy as np
from jax import lax
from jax.sharding import PartitionSpec as P

STEPS = 4
COARSE_STEPS = STEPS // 4


def advance(field, conduct, absorb, diffuse_scale, react_scale):
    center = field[1:-1]
    middle = conduct[1:-1]
    padded = jnp.pad(center, ((0, 0), (1, 1), (1, 1)))
    conduct_pad = jnp.pad(middle, ((0, 0), (1, 1), (1, 1)))
    inflow = 0.5 * (conduct[2:] + middle) * (field[2:] - center)
    inflow = inflow + 0.5 * (conduct[:-2] + middle) * (field[:-2] - center)
    inflow = inflow + 0.5 * (conduct_pad[:, 2:, 1:-1] + middle) * (padded[:, 2:, 1:-1] - center)
    inflow = inflow + 0.5 * (conduct_pad[:, :-2, 1:-1] + middle) * (padded[:, :-2, 1:-1] - center)
    inflow = inflow + 0.5 * (conduct_pad[:, 1:-1, 2:] + middle) * (padded[:, 1:-1, 2:] - center)
    inflow = inflow + 0.5 * (conduct_pad[:, 1:-1, :-2] + middle) * (padded[:, 1:-1, :-2] - center)
    return center + diffuse_scale * inflow - react_scale * absorb[1:-1] * center


def pair_matrix(fine):
    rows = np.arange(fine)[:, None] // 2 == np.arange(fine // 2)[None, :]
    return jnp.asarray(rows.astype(np.float32))


def restrict(field):
    first, second, third = field.shape
    planes = field.reshape(first // 2, 2, second, third).sum(axis=1)
    rows = pair_matrix(second)
    cols = pair_matrix(third)
    out = jnp.einsum("Yy,mYZ,Zz->myz", rows, planes, cols, precision=lax.Precision.HIGHEST)
    return out * 0.125


def prolong(field):
    first, second, third = field.shape
    rows = pair_matrix(second * 2)
    cols = pair_matrix(third * 2)
    out = jnp.einsum("Yy,myz,Zz->mYZ", rows, field, cols, precision=lax.Precision.HIGHEST)
    return jnp.repeat(out, 2, axis=0)


def gather_planes(block, axis_names, pairs_of, distances):
    pieces = {}
    for d in distances:
        if d == 0 and pairs_of(0) is None:
            pieces[d] = block
            continue
        pieces[d] = lax.ppermute(block, axis_names, pairs_of(d))
    return pieces


def shards(initial, guesses, diffusivity, reaction):
    space = lax.axis_size("space")
    times = lax.axis_size("tm")
    me_s = lax.axis_index("space")
    me_t = lax.axis_index("tm")
    n = initial.shape[0]
    halo = STEPS
    reach = -(-halo // n)

    def space_pairs(d):
        return [(s + d, s) for s in range(space) if 0 <= s + d < space]

    def joint(s, t):
        return s * times + t

    def prev_pairs(d):
        return [
            (joint(s + d, (t - 1) % times), joint(s, t))
            for s in range(space)
            for t in range(times)
            if 0 <= s + d < space
        ]

    start = guesses[0]
    distances = [d for d in range(-reach, reach + 1)]
    lo = reach * n - halo
    hi = reach * n + n + halo
    split = times % 2 == 0
    if split:
        even = me_t % 2 == 0
        local = jnp.where(even, jnp.stack([diffusivity, start]), jnp.stack([reaction, start]))
    else:
        local = jnp.stack([diffusivity, reaction, start])
    got = gather_planes(local, "space", lambda d: None if d == 0 else space_pairs(d), distances)
    wide = jnp.concatenate([got[d] for d in distances], axis=1)
    wide = wide[:, lo:hi]
    if split:
        mine = wide[0]
        rim = jnp.concatenate([mine[:halo], mine[halo + n :]], axis=0)
        partner = [(t, t ^ 1) for t in range(times)]
        theirs_rim = lax.ppermute(rim, "tm", partner)
        theirs_own = jnp.where(even, reaction, diffusivity)
        theirs = jnp.concatenate([theirs_rim[:halo], theirs_own, theirs_rim[halo:]], axis=0)
        conduct = jnp.where(even, mine, theirs)
        absorb = jnp.where(even, theirs, mine)
        field0 = wide[1]
    else:
        conduct, absorb, field0 = wide[0], wide[1], wide[2]
    plane_ids = me_s * n - halo + jnp.arange(n + 2 * halo)
    inside = ((plane_ids >= 0) & (plane_ids < space * n)).astype(jnp.float32)[:, None, None]

    def fine_prop(field, first_step=0):
        for number in range(first_step, STEPS):
            cut = number
            k = conduct[cut : conduct.shape[0] - cut]
            c = absorb[cut : absorb.shape[0] - cut]
            field = advance(field, k, c, 0.1, 0.1)
            if number < STEPS - 1:
                m = inside[cut + 1 : inside.shape[0] - cut - 1]
                field = jnp.where(m > 0, field, 0.0)
        return field

    advanced = fine_prop(field0)
    payload = jnp.where(me_t == times - 1, initial, advanced)
    got2 = gather_planes(payload, ("space", "tm"), prev_pairs, distances)
    if lo == 0 and n == 2 and halo == 4:
        blocks = [got2[d] for d in distances]
        flat = [blk[i] for blk in blocks for i in range(n)]
        outs = []
        for p0, p1 in [(1, 2), (2, 4), (4, 6), (6, 8), (8, 9)]:
            window = jnp.stack(flat[p0 - 1 : p1 + 1])
            piece = advance(window, conduct[p0 - 1 : p1 + 1], absorb[p0 - 1 : p1 + 1], 0.1, 0.1)
            outs.append(jnp.where(inside[p0:p1] > 0, piece, 0.0))
        residual = fine_prop(jnp.concatenate(outs, axis=0), first_step=1) - advanced
    else:
        relaxed = jnp.concatenate([got2[d] for d in distances], axis=0)[lo:hi]
        residual = fine_prop(relaxed) - advanced

    cn = n // 2
    creach = -(-1 // cn)
    cdist = [d for d in range(-creach, creach + 1)]
    coarse_k = restrict(conduct[halo - 2 * creach * cn : halo + n + 2 * creach * cn])
    coarse_c = restrict(absorb[halo - 2 * creach * cn : halo + n + 2 * creach * cn])
    ck = coarse_k[creach * cn - 1 : creach * cn + cn + 1]
    cc = coarse_c[creach * cn - 1 : creach * cn + cn + 1]
    source = restrict(residual)

    def chain_pairs(d):
        return [
            (joint(s + d, t - 1), joint(s, t))
            for s in range(space)
            for t in range(1, times)
            if 0 <= s + d < space
        ]

    partial_error = source
    for turn in range(times - 1):
        got3 = gather_planes(partial_error, ("space", "tm"), chain_pairs, cdist)
        behind = jnp.concatenate([got3[d] for d in cdist], axis=0)
        behind = behind[creach * cn - 1 : creach * cn + cn + 1]
        for number in range(COARSE_STEPS):
            behind = advance(behind, ck, cc, 0.1, 0.4)
        partial_error = source + behind
    corrected = advanced + prolong(partial_error)
    return (corrected[None], residual[None])


def solution(mesh):
    in_specs = (
        P("space", None, None),
        P("tm", "space", None, None),
        P("space", None, None),
        P("space", None, None),
    )
    out_specs = (P("tm", "space", None, None), P("tm", "space", None, None))
    return jax.shard_map(shards, mesh=mesh, in_specs=in_specs, out_specs=out_specs, check_vma=False)
```

```python
import jax
import jax.numpy as jnp
import numpy as np
from jax import lax
from jax.sharding import PartitionSpec as P

STEPS = 4
COARSE_STEPS = STEPS // 4


def advance(field, conduct, absorb, diffuse_scale, react_scale):
    center = field[1:-1]
    middle = conduct[1:-1]
    padded = jnp.pad(center, ((0, 0), (1, 1), (1, 1)))
    conduct_pad = jnp.pad(middle, ((0, 0), (1, 1), (1, 1)))
    inflow = 0.5 * (conduct[2:] + middle) * (field[2:] - center)
    inflow = inflow + 0.5 * (conduct[:-2] + middle) * (field[:-2] - center)
    inflow = inflow + 0.5 * (conduct_pad[:, 2:, 1:-1] + middle) * (padded[:, 2:, 1:-1] - center)
    inflow = inflow + 0.5 * (conduct_pad[:, :-2, 1:-1] + middle) * (padded[:, :-2, 1:-1] - center)
    inflow = inflow + 0.5 * (conduct_pad[:, 1:-1, 2:] + middle) * (padded[:, 1:-1, 2:] - center)
    inflow = inflow + 0.5 * (conduct_pad[:, 1:-1, :-2] + middle) * (padded[:, 1:-1, :-2] - center)
    return center + diffuse_scale * inflow - react_scale * absorb[1:-1] * center


def pair_matrix(fine):
    rows = np.arange(fine)[:, None] // 2 == np.arange(fine // 2)[None, :]
    return jnp.asarray(rows.astype(np.float32))


def restrict(field):
    first, second, third = field.shape
    planes = field.reshape(first // 2, 2, second, third).sum(axis=1)
    rows = pair_matrix(second)
    cols = pair_matrix(third)
    out = jnp.einsum("Yy,mYZ,Zz->myz", rows, planes, cols, precision=lax.Precision.HIGHEST)
    return out * 0.125


def prolong(field):
    first, second, third = field.shape
    rows = pair_matrix(second * 2)
    cols = pair_matrix(third * 2)
    out = jnp.einsum("Yy,myz,Zz->mYZ", rows, field, cols, precision=lax.Precision.HIGHEST)
    return jnp.repeat(out, 2, axis=0)


def gather_planes(block, axis_names, pairs_of, distances):
    pieces = {}
    for d in distances:
        if d == 0 and pairs_of(0) is None:
            pieces[d] = block
            continue
        pieces[d] = lax.ppermute(block, axis_names, pairs_of(d))
    return pieces


def shards(initial, guesses, diffusivity, reaction):
    space = lax.axis_size("space")
    times = lax.axis_size("tm")
    me_s = lax.axis_index("space")
    me_t = lax.axis_index("tm")
    n = initial.shape[0]
    halo = STEPS
    reach = -(-halo // n)

    def space_pairs(d):
        return [(s + d, s) for s in range(space) if 0 <= s + d < space]

    def joint(s, t):
        return s * times + t

    def prev_pairs(d):
        return [
            (joint(s + d, (t - 1) % times), joint(s, t))
            for s in range(space)
            for t in range(times)
            if 0 <= s + d < space
        ]

    start = guesses[0]
    distances = [d for d in range(-reach, reach + 1)]
    lo = reach * n - halo
    hi = reach * n + n + halo
    split = times % 2 == 0
    if split:
        even = me_t % 2 == 0
        local = jnp.where(even, jnp.stack([diffusivity, start]), jnp.stack([reaction, start]))
    else:
        local = jnp.stack([diffusivity, reaction, start])
    got = gather_planes(local, "space", lambda d: None if d == 0 else space_pairs(d), distances)
    wide = jnp.concatenate([got[d] for d in distances], axis=1)
    wide = wide[:, lo:hi]
    if split:
        mine = wide[0]
        partner = [(t, t ^ 1) for t in range(times)]
        theirs = lax.ppermute(mine, "tm", partner)
        conduct = jnp.where(even, mine, theirs)
        absorb = jnp.where(even, theirs, mine)
        field0 = wide[1]
    else:
        conduct, absorb, field0 = wide[0], wide[1], wide[2]
    plane_ids = me_s * n - halo + jnp.arange(n + 2 * halo)
    inside = ((plane_ids >= 0) & (plane_ids < space * n)).astype(jnp.float32)[:, None, None]

    def fine_prop(field):
        for number in range(STEPS):
            cut = number
            k = conduct[cut : conduct.shape[0] - cut]
            c = absorb[cut : absorb.shape[0] - cut]
            field = advance(field, k, c, 0.1, 0.1)
            if number < STEPS - 1:
                m = inside[cut + 1 : inside.shape[0] - cut - 1]
                field = jnp.where(m > 0, field, 0.0)
        return field

    advanced = fine_prop(field0)
    payload = jnp.where(me_t == times - 1, initial, advanced)
    got2 = gather_planes(payload, ("space", "tm"), prev_pairs, distances)
    relaxed = jnp.concatenate([got2[d] for d in distances], axis=0)[lo:hi]
    residual = fine_prop(relaxed) - advanced

    cn = n // 2
    creach = -(-1 // cn)
    cdist = [d for d in range(-creach, creach + 1)]
    coarse_k = restrict(conduct[halo - 2 * creach * cn : halo + n + 2 * creach * cn])
    coarse_c = restrict(absorb[halo - 2 * creach * cn : halo + n + 2 * creach * cn])
    ck = coarse_k[creach * cn - 1 : creach * cn + cn + 1]
    cc = coarse_c[creach * cn - 1 : creach * cn + cn + 1]
    source = restrict(residual)

    def chain_pairs(d):
        return [
            (joint(s + d, t - 1), joint(s, t))
            for s in range(space)
            for t in range(1, times)
            if 0 <= s + d < space
        ]

    partial_error = source
    for turn in range(times - 1):
        got3 = gather_planes(partial_error, ("space", "tm"), chain_pairs, cdist)
        behind = jnp.concatenate([got3[d] for d in cdist], axis=0)
        behind = behind[creach * cn - 1 : creach * cn + cn + 1]
        for number in range(COARSE_STEPS):
            behind = advance(behind, ck, cc, 0.1, 0.4)
        partial_error = source + behind
    corrected = advanced + prolong(partial_error)
    return (corrected[None], residual[None])


def solution(mesh):
    in_specs = (
        P("space", None, None),
        P("tm", "space", None, None),
        P("space", None, None),
        P("space", None, None),
    )
    out_specs = (P("tm", "space", None, None), P("tm", "space", None, None))
    return jax.shard_map(shards, mesh=mesh, in_specs=in_specs, out_specs=out_specs, check_vma=False)
```

```python
import jax
import jax.numpy as jnp
import numpy as np
from jax import lax
from jax.sharding import PartitionSpec as P

STEPS = 4
COARSE_STEPS = STEPS // 4


def advance(field, conduct, absorb, diffuse_scale, react_scale):
    center = field[1:-1]
    middle = conduct[1:-1]
    padded = jnp.pad(center, ((0, 0), (1, 1), (1, 1)))
    conduct_pad = jnp.pad(middle, ((0, 0), (1, 1), (1, 1)))
    inflow = 0.5 * (conduct[2:] + middle) * (field[2:] - center)
    inflow = inflow + 0.5 * (conduct[:-2] + middle) * (field[:-2] - center)
    inflow = inflow + 0.5 * (conduct_pad[:, 2:, 1:-1] + middle) * (padded[:, 2:, 1:-1] - center)
    inflow = inflow + 0.5 * (conduct_pad[:, :-2, 1:-1] + middle) * (padded[:, :-2, 1:-1] - center)
    inflow = inflow + 0.5 * (conduct_pad[:, 1:-1, 2:] + middle) * (padded[:, 1:-1, 2:] - center)
    inflow = inflow + 0.5 * (conduct_pad[:, 1:-1, :-2] + middle) * (padded[:, 1:-1, :-2] - center)
    return center + diffuse_scale * inflow - react_scale * absorb[1:-1] * center


def pair_matrix(fine):
    rows = np.arange(fine)[:, None] // 2 == np.arange(fine // 2)[None, :]
    return jnp.asarray(rows.astype(np.float32))


def restrict(field):
    first, second, third = field.shape
    planes = field.reshape(first // 2, 2, second, third).sum(axis=1)
    rows = pair_matrix(second)
    cols = pair_matrix(third)
    out = jnp.einsum("Yy,mYZ,Zz->myz", rows, planes, cols, precision=lax.Precision.HIGHEST)
    return out * 0.125


def prolong(field):
    first, second, third = field.shape
    rows = pair_matrix(second * 2)
    cols = pair_matrix(third * 2)
    out = jnp.einsum("Yy,myz,Zz->mYZ", rows, field, cols, precision=lax.Precision.HIGHEST)
    return jnp.repeat(out, 2, axis=0)


def gather_planes(block, axis_names, pairs_of, distances):
    pieces = {}
    for d in distances:
        if d == 0 and pairs_of(0) is None:
            pieces[d] = block
            continue
        pieces[d] = lax.ppermute(block, axis_names, pairs_of(d))
    return pieces


def shards(initial, guesses, diffusivity, reaction):
    space = lax.axis_size("space")
    times = lax.axis_size("tm")
    me_s = lax.axis_index("space")
    me_t = lax.axis_index("tm")
    n = initial.shape[0]
    halo = STEPS
    reach = -(-halo // n)

    def space_pairs(d):
        return [(s + d, s) for s in range(space) if 0 <= s + d < space]

    def joint(s, t):
        return s * times + t

    def prev_pairs(d):
        return [
            (joint(s + d, (t - 1) % times), joint(s, t))
            for s in range(space)
            for t in range(times)
            if 0 <= s + d < space
        ]

    start = guesses[0]
    distances = [d for d in range(-reach, reach + 1)]
    lo = reach * n - halo
    hi = reach * n + n + halo
    split = times % 2 == 0
    if split:
        even = me_t % 2 == 0
        local = jnp.where(even, jnp.stack([diffusivity, start]), jnp.stack([reaction, start]))
    else:
        local = jnp.stack([diffusivity, reaction, start])
    got = gather_planes(local, "space", lambda d: None if d == 0 else space_pairs(d), distances)
    wide = jnp.concatenate([got[d] for d in distances], axis=1)
    wide = wide[:, lo:hi]
    if split:
        mine = wide[0]
        rim = jnp.concatenate([mine[:halo], mine[halo + n :]], axis=0)
        partner = [(t, t ^ 1) for t in range(times)]
        theirs_rim = lax.ppermute(rim, "tm", partner)
        theirs_own = jnp.where(even, reaction, diffusivity)
        theirs = jnp.concatenate([theirs_rim[:halo], theirs_own, theirs_rim[halo:]], axis=0)
        conduct = jnp.where(even, mine, theirs)
        absorb = jnp.where(even, theirs, mine)
        field0 = wide[1]
    else:
        conduct, absorb, field0 = wide[0], wide[1], wide[2]
    plane_ids = me_s * n - halo + jnp.arange(n + 2 * halo)
    inside = ((plane_ids >= 0) & (plane_ids < space * n)).astype(jnp.float32)[:, None, None]

    def fine_prop(field, steps=STEPS):
        for number in range(steps):
            cut = number
            k = conduct[cut : conduct.shape[0] - cut]
            c = absorb[cut : absorb.shape[0] - cut]
            field = advance(field, k, c, 0.1, 0.1)
            if number < STEPS - 1:
                m = inside[cut + 1 : inside.shape[0] - cut - 1]
                field = jnp.where(m > 0, field, 0.0)
        return field

    before_last = fine_prop(field0, STEPS - 1)
    last_k = conduct[STEPS - 1 : conduct.shape[0] - STEPS + 1]
    last_c = absorb[STEPS - 1 : absorb.shape[0] - STEPS + 1]
    payload = jnp.where(me_t == times - 1, initial, advance(before_last, last_k, last_c, 0.1, 0.1))
    kept = lax.optimization_barrier(before_last)
    advanced = advance(kept, last_k, last_c, 0.1, 0.1)
    got2 = gather_planes(payload, ("space", "tm"), prev_pairs, distances)
    relaxed = jnp.concatenate([got2[d] for d in distances], axis=0)[lo:hi]
    residual = fine_prop(relaxed) - advanced

    cn = n // 2
    creach = -(-1 // cn)
    cdist = [d for d in range(-creach, creach + 1)]
    coarse_k = restrict(conduct[halo - 2 * creach * cn : halo + n + 2 * creach * cn])
    coarse_c = restrict(absorb[halo - 2 * creach * cn : halo + n + 2 * creach * cn])
    ck = coarse_k[creach * cn - 1 : creach * cn + cn + 1]
    cc = coarse_c[creach * cn - 1 : creach * cn + cn + 1]
    source = restrict(residual)

    def chain_pairs(d):
        return [
            (joint(s + d, t - 1), joint(s, t))
            for s in range(space)
            for t in range(1, times)
            if 0 <= s + d < space
        ]

    partial_error = source
    for turn in range(times - 1):
        got3 = gather_planes(partial_error, ("space", "tm"), chain_pairs, cdist)
        behind = jnp.concatenate([got3[d] for d in cdist], axis=0)
        behind = behind[creach * cn - 1 : creach * cn + cn + 1]
        for number in range(COARSE_STEPS):
            behind = advance(behind, ck, cc, 0.1, 0.4)
        partial_error = source + behind
    corrected = advanced + prolong(partial_error)
    return (corrected[None], residual[None])


def solution(mesh):
    in_specs = (
        P("space", None, None),
        P("tm", "space", None, None),
        P("space", None, None),
        P("space", None, None),
    )
    out_specs = (P("tm", "space", None, None), P("tm", "space", None, None))
    return jax.shard_map(shards, mesh=mesh, in_specs=in_specs, out_specs=out_specs, check_vma=False)
```
